128 devices in a mesh: ep: 32 (over x, y, core), tp: 4 (over z).
Axes of the slice: x: 4, y: 4, z: 4, core: 2. Of those that a mesh axis runs over, the one named last changes fastest.
Arguments:
- query: bfloat16 [3, 1024, 8192], P(None, 'ep', 'tp'), may hold values from -110 to 110
- step_key_value: bfloat16 [3, 2, 1024, 512], P(None, None, 'ep', 'tp'), may hold values from -5 to 5
- key_value_cache: bfloat16 [2, 1024, 128, 512], P(None, 'ep', None, 'tp'), may hold values from -5 to 5
- lengths: int32 [1024], P('ep'), may hold values from 2 to 128, as said below
- hidden_in: bfloat16 [3, 1024, 4096], P(None, ('ep', 'tp')), may hold values from -3 to 3
- norm_gain: float32 [4096], replicated, may hold values from 0.5 to 1.5
- w_out: bfloat16 [8192, 4096], P('tp', 'ep'), may hold values from -0.1875 to 0.1875
- routes: int32 [3, 1024, 8], P(None, ('ep', 'tp')), may hold values from 0 to 127, all different within a row; in each aligned block of 8 rows (0 to 7, 8 to 15, ..., all dimensions but the last counted through in order) at most 2 rows name the same one
- gate_scores: float32 [3, 1024, 8], P(None, ('ep', 'tp')), may hold values from 0.1 to 1
- expert_gate: bfloat16 [128, 4096, 768], P(('ep', 'tp')), may hold values from -0.09375 to 0.09375
- expert_up: bfloat16 [128, 4096, 768], P(('ep', 'tp')), may hold values from -0.09375 to 0.09375
- expert_down: bfloat16 [128, 768, 4096], P(('ep', 'tp')), may hold values from -0.21875 to 0.21875
Outputs:
- layer_out: bfloat16 [3, 1024, 4096], P(None, ('ep', 'tp'))
The draws below stay inside these ranges and needn't reach their ends.
Inputs may be any that keep to these rules, and one draw needn't show every extreme that they name: `lengths`: every row has at least two filled cache positions, and some row fills all 128. `routes`: A row names 8 different experts. Within one step, the 8 rows of one device (aligned blocks of rows) name any one expert at most 2 times.
All inputs are finite; a program needn't handle non-finite values.
Results may differ from the reference program's by a relative error of at most 0.007.
Values may be sent and summed in bfloat16 or wider, within the bound.
No kernel may reach another device: no remote copies, remote signals or barrier semaphores. Data moves between devices by JAX's collectives and lax.ppermute only.
A program may use at most 128 MiB of HBM per device.

```python
import math
import jax
import jax.numpy as jnp
import numpy as np
from jax import lax

D = 4096
QUERY_HEADS = 64
KEY_VALUE_HEADS = 4
HEAD_SIZE = 128
TOPK = 8
FFW = 768
DECODE_STEPS = 3
CACHE_POSITIONS = 128
ROW_OWN = 8
CAP = 2
TOTAL_ROWS = 1024
EXPERTS = 128
N_EP = 32
N_TP = 4


def draw_key_value_cache(key, part):
    base_offset = jnp.clip(jax.random.normal(jax.random.fold_in(key, 11), (2, TOTAL_ROWS, CACHE_POSITIONS, KEY_VALUE_HEADS * HEAD_SIZE), jnp.float32), -5.0, 5.0)
    return base_offset.astype(jnp.bfloat16)


def draw_query(key, part):
    base_offset = jnp.clip(jax.random.normal(jax.random.fold_in(key, 13), (DECODE_STEPS, TOTAL_ROWS, QUERY_HEADS * HEAD_SIZE), jnp.float32), -5.0, 5.0)
    return base_offset.astype(jnp.bfloat16)


def draw_lengths(key, part):
    filled = jax.random.randint(jax.random.fold_in(key, 7), (TOTAL_ROWS,), 2, CACHE_POSITIONS + 1, jnp.int32)
    filled = filled.at[0].set(CACHE_POSITIONS)
    filled = filled.at[1].set(2)
    return filled


def shard_levels(rng, shape, shards, smallest, top_value):
    loudness = 1.0
    for position, blocks in shards:
        steps = jax.random.uniform(jax.random.fold_in(jax.random.fold_in(rng, 6), position), (blocks,), jnp.float32, smallest / len(shards), top_value / len(shards))
        loudness = loudness * jnp.repeat(jnp.exp(steps), shape[position] // blocks).reshape((-1,) + (1,) * (len(shape) - 1 - position))
    return loudness


def assign_block(rng, own, number, rows, number_of, top, limit, slope):
    order = jax.random.permutation(rng, number_of)
    packed, usual = portions_of(number_of, rows * top, limit, slope, True), portions_of(number_of, rows * top, limit, slope, False)
    places = jnp.arange(number_of)

    def named(tallies, rotation):
        used = int((tallies > 0).sum())
        fixed = max(1, used // 4)
        shifted = fixed + (places - fixed + rotation * (used - fixed)) % max(1, number_of - fixed)
        return jnp.zeros((number_of,), jnp.int32).at[order[jnp.where(places < fixed, places, shifted)]].set(jnp.asarray(tallies, jnp.int32))

    tallies = jnp.where(number % 4 == 0, named(packed, number // 4), named(usual, number - number // 4 - 1))
    mixed = jax.random.permutation(jax.random.fold_in(own, 3), number_of)
    source_of, receiver = mixed[0:number_of // 2 * 2:2], mixed[1:number_of // 2 * 2:2]
    room = jnp.minimum(tallies[source_of] - 1, limit - tallies[receiver]) // 2
    room = jnp.where((source_of == order[0]) | (receiver == order[0]) | (tallies[receiver] == 0), 0, jnp.maximum(room, 0))
    shifted = jax.random.randint(jax.random.fold_in(own, 4), (number_of // 2,), 0, 1 << 20) % (room + 1)
    tallies = tallies.at[source_of].add(-shifted).at[receiver].add(shifted)
    items = jnp.searchsorted(jnp.cumsum(tallies), jnp.arange(rows * top), side="right").astype(jnp.int32)
    listing = items.reshape(top, rows).T
    listing = listing[jax.random.permutation(jax.random.fold_in(own, 1), rows)]
    rotation = jax.random.randint(jax.random.fold_in(own, 2), (rows, 1), 0, top)
    return jnp.take_along_axis(listing, (jnp.arange(top)[None, :] + rotation) % top, axis=1)


def portions_of(amount, total, reach, slope, full):
    loads = [(1 << 20) // math.isqrt(grade ** slope) + 1 for grade in range(1, amount + 1)]
    largest = reach if full else min(reach, max(-(-total // amount), total * loads[0] // sum(loads)))
    least = 1 if total - largest >= amount - 1 else 0
    holding, surplus = [largest] + [least] * (amount - 1), total - largest - least * (amount - 1)
    while surplus > 0:
        movable = [i for i in range(1, amount) if holding[i] < largest] or [i for i in range(1, amount) if holding[i] < reach]
        mass, budget = sum([loads[i] for i in movable]), surplus
        for i in movable:
            addition = min(reach - holding[i], max(1, budget * loads[i] // mass), surplus)
            holding[i] = holding[i] + addition
            surplus = surplus - addition
    return np.array(holding)


def noise(stream_key, extent, width, reach, pieces=(), kind=jnp.bfloat16):
    result = width * jax.random.normal(stream_key, extent, jnp.float32)
    if pieces:
        result = result * shard_levels(stream_key, extent, pieces, -0.22, 0.18)
    return jnp.clip(result, -reach, reach).astype(kind)


def setup_inputs(seed: int = 0) -> dict:
    key_list = jax.random.split(jax.random.key(seed), 13)
    query = draw_query(jax.random.fold_in(key_list[12], 71), 0)
    step_key_value = noise(key_list[1], (DECODE_STEPS, 2, TOTAL_ROWS, KEY_VALUE_HEADS * HEAD_SIZE), 1.0, 5.0, ((2, 32), (3, 4)))
    key_value_cache = draw_key_value_cache(jax.random.fold_in(key_list[12], 71), 0)
    lengths = draw_lengths(jax.random.fold_in(key_list[12], 71), 0)
    hidden_in = noise(key_list[4], (DECODE_STEPS, TOTAL_ROWS, D), 0.5, 3.0, ((1, 128),))
    norm_gain = jnp.clip(1.0 + 0.1 * jax.random.normal(key_list[5], (D,), jnp.float32), 0.5, 1.5)
    w_out = noise(key_list[6], (QUERY_HEADS * HEAD_SIZE, D), (QUERY_HEADS * HEAD_SIZE // 8) ** -0.5, 0.1875, ((0, 4), (1, 32)))
    routes_keys = jax.random.split(jax.random.fold_in(key_list[7], 1), DECODE_STEPS * TOTAL_ROWS // ROW_OWN)
    routes_turns = jax.random.permutation(jax.random.fold_in(key_list[7], 3), DECODE_STEPS * TOTAL_ROWS // ROW_OWN)
    routes = jax.vmap(lambda own, number: assign_block(jax.random.fold_in(key_list[7], 2), own, number, ROW_OWN, EXPERTS, TOPK, CAP, 2))(routes_keys, routes_turns).reshape((DECODE_STEPS, TOTAL_ROWS, TOPK))
    gate_scores = jnp.clip(0.1 + 0.9 * jax.random.uniform(key_list[8], (DECODE_STEPS, TOTAL_ROWS, TOPK), jnp.float32) ** shard_levels(key_list[8], (DECODE_STEPS, TOTAL_ROWS, TOPK), ((1, 128),), -0.2, 0.2), 0.1, 1.0)
    expert_gate = noise(key_list[9], (EXPERTS, D, FFW), D ** -0.5, 0.09375, ((0, 128),))
    expert_up = noise(key_list[10], (EXPERTS, D, FFW), D ** -0.5, 0.09375, ((0, 128),))
    expert_down = noise(key_list[11], (EXPERTS, FFW, D), FFW ** -0.5, 0.21875, ((0, 128),))
    return dict(query=query, step_key_value=step_key_value, key_value_cache=key_value_cache, lengths=lengths, hidden_in=hidden_in, norm_gain=norm_gain, w_out=w_out, routes=routes, gate_scores=gate_scores, expert_gate=expert_gate, expert_up=expert_up, expert_down=expert_down)


masked_score = -1e+30
norm_eps = 1e-06

def mix_experts(normed, route_ids, weights, expert_gate, expert_up, expert_down):
    flat_ids = route_ids.reshape(-1)
    flat_weights = weights.reshape(-1)
    most_rows = N_EP * N_TP * CAP
    block_rows = min(64, most_rows)

    def per_expert(total, inputs):
        expert, gate_weights, up_weights, down_weights = inputs
        matches = flat_ids == expert
        count = jnp.sum(matches.astype(jnp.int32))
        order = jnp.nonzero(matches, size=most_rows, fill_value=0)[0].astype(jnp.int32)

        def one_block(index, running):
            picked = lax.dynamic_slice_in_dim(order, (index * block_rows).astype(jnp.int32), block_rows)
            live = index * block_rows + jnp.arange(block_rows, dtype=jnp.int32) < count
            row_ids = picked // TOPK
            inputs_rows = normed[row_ids]
            gate_act = jnp.dot(inputs_rows, gate_weights, preferred_element_type=jnp.float32)
            up_act = jnp.dot(inputs_rows, up_weights, preferred_element_type=jnp.float32)
            hidden = (jax.nn.silu(gate_act) * up_act).astype(jnp.bfloat16)
            expert_out = jnp.dot(hidden, down_weights, preferred_element_type=jnp.float32).astype(jnp.bfloat16)
            scaled = jnp.where(live, flat_weights[picked], jnp.zeros_like(flat_weights[picked]))
            return running.at[row_ids].add(scaled[:, None] * expert_out.astype(jnp.float32))
        blocks = (count + block_rows - 1) // block_rows
        total = lax.fori_loop(jnp.int32(0), blocks.astype(jnp.int32), one_block, total)
        return (total, None)
    start = jnp.zeros((normed.shape[0], D), jnp.float32)
    experts_list = jnp.arange(EXPERTS, dtype=jnp.int32)
    total, _ = lax.scan(per_expert, start, (experts_list, expert_gate, expert_up, expert_down))
    return total

def reference(query, step_key_value, key_value_cache, lengths, hidden_in, norm_gain, w_out, routes, gate_scores, expert_gate, expert_up, expert_down):
    query_group = QUERY_HEADS // KEY_VALUE_HEADS
    score_scale = HEAD_SIZE ** (-0.5)
    stored_keys = key_value_cache[0].astype(jnp.float32).reshape(TOTAL_ROWS, CACHE_POSITIONS, KEY_VALUE_HEADS, HEAD_SIZE)
    stored_values = key_value_cache[1].astype(jnp.float32).reshape(TOTAL_ROWS, CACHE_POSITIONS, KEY_VALUE_HEADS, HEAD_SIZE)
    usable = jnp.arange(CACHE_POSITIONS, dtype=jnp.int32)[None, :] < lengths[:, None]
    results = []
    for decode_step in range(DECODE_STEPS):
        query_rows = query[decode_step].astype(jnp.float32).reshape(TOTAL_ROWS, KEY_VALUE_HEADS, query_group, HEAD_SIZE)
        incoming_keys = step_key_value[:decode_step + 1, 0].astype(jnp.float32).reshape(decode_step + 1, TOTAL_ROWS, KEY_VALUE_HEADS, HEAD_SIZE)
        incoming_values = step_key_value[:decode_step + 1, 1].astype(jnp.float32).reshape(decode_step + 1, TOTAL_ROWS, KEY_VALUE_HEADS, HEAD_SIZE)
        cache_scores = jnp.einsum('rgqd,rjgd->rgqj', query_rows, stored_keys) * score_scale
        cache_scores = jnp.where(usable[:, None, None, :], cache_scores, masked_score)
        fresh_scores = jnp.einsum('rgqd,jrgd->rgqj', query_rows, incoming_keys) * score_scale
        scores = jnp.concatenate([cache_scores, fresh_scores], axis=-1)
        top = lax.optimization_barrier(jnp.max(scores, axis=-1, keepdims=True))
        raised = jnp.exp(scores - top)
        probs = (raised / lax.optimization_barrier(jnp.sum(raised, axis=-1, keepdims=True))).astype(jnp.bfloat16)
        probs_wide = probs.astype(jnp.float32)
        attended = jnp.einsum('rgqj,rjgd->rgqd', probs_wide[..., :CACHE_POSITIONS], stored_values)
        attended = attended + jnp.einsum('rgqj,jrgd->rgqd', probs_wide[..., CACHE_POSITIONS:], incoming_values)
        attended = attended.astype(jnp.bfloat16).reshape(TOTAL_ROWS, QUERY_HEADS * HEAD_SIZE)
        projected = jnp.dot(attended, w_out, preferred_element_type=jnp.float32).astype(jnp.bfloat16)
        residual = hidden_in[decode_step].astype(jnp.float32) + projected.astype(jnp.float32)
        mean_square = lax.optimization_barrier(jnp.mean(residual * residual, axis=-1, keepdims=True))
        normed = (residual * lax.rsqrt(mean_square + norm_eps) * norm_gain).astype(jnp.bfloat16)
        weights = gate_scores[decode_step] / lax.optimization_barrier(jnp.sum(gate_scores[decode_step], axis=-1, keepdims=True))
        expert_mix = mix_experts(normed, routes[decode_step], weights, expert_gate, expert_up, expert_down)
        results.append((residual + expert_mix).astype(jnp.bfloat16))
    return jnp.stack(results)
```

```python
import jax
import jax.numpy as jnp
from jax import lax
from jax.sharding import PartitionSpec as P

HEAD_SIZE = 128
TOPK = 8
SLOTS = 256
DECODE_STEPS = 3


masked_score = -1e30
norm_eps = 1e-06


def per_device(
    query,
    step_key_value,
    key_value_cache,
    lengths,
    hidden_in,
    norm_gain,
    w_out,
    routes,
    gate_scores,
    expert_gate,
    expert_up,
    expert_down,
):
    ep_count = lax.axis_size("ep")
    tp_count = lax.axis_size("tp")
    steps = query.shape[0]
    row_dev = query.shape[1]
    row_own = hidden_in.shape[1]
    width = hidden_in.shape[2]
    heads_dev = query.shape[2] // HEAD_SIZE
    cache_len = key_value_cache.shape[2]
    expert_count = ep_count * tp_count * expert_gate.shape[0]
    capacity = SLOTS // expert_count
    score_scale = HEAD_SIZE ** (-0.5)
    stored_keys = key_value_cache[0]
    stored_values = key_value_cache[1]
    usable = jnp.arange(cache_len, dtype=jnp.int32)[None, :] < lengths[:, None]

    query_rows = query.reshape(steps, row_dev, heads_dev, HEAD_SIZE)
    incoming_keys = step_key_value[:, 0]
    incoming_values = step_key_value[:, 1]
    cache_scores = (
        jnp.einsum("srhd,rjd->srhj", query_rows, stored_keys, preferred_element_type=jnp.float32)
        * score_scale
    )
    cache_scores = jnp.where(usable[None, :, None, :], cache_scores, masked_score)
    fresh_scores = (
        jnp.einsum("srhd,jrd->srhj", query_rows, incoming_keys, preferred_element_type=jnp.float32)
        * score_scale
    )
    fresh_ok = (
        jnp.arange(steps, dtype=jnp.int32)[None, :] <= jnp.arange(steps, dtype=jnp.int32)[:, None]
    )
    fresh_scores = jnp.where(fresh_ok[:, None, None, :], fresh_scores, masked_score)
    scores = jnp.concatenate([cache_scores, fresh_scores], axis=-1)
    top = jnp.max(scores, axis=-1, keepdims=True)
    raised = jnp.exp(scores - top)
    probs = (raised / jnp.sum(raised, axis=-1, keepdims=True)).astype(jnp.bfloat16)
    attended = jnp.einsum(
        "srhj,rjd->srhd", probs[..., :cache_len], stored_values, preferred_element_type=jnp.float32
    )
    attended = attended + jnp.einsum(
        "srhj,jrd->srhd", probs[..., cache_len:], incoming_values, preferred_element_type=jnp.float32
    )
    attended = attended.astype(jnp.bfloat16).reshape(steps, row_dev, heads_dev * HEAD_SIZE)

    gathered = lax.all_gather(attended, "ep", axis=1, tiled=True)
    partial_sums = jnp.einsum(
        "srk,kc->src", gathered, w_out, preferred_element_type=jnp.float32
    )
    grouped = partial_sums.reshape(steps, ep_count * tp_count, row_own, -1)
    arrived_sums = lax.all_to_all(
        grouped, ("ep", "tp"), split_axis=1, concat_axis=1, tiled=True
    )
    arrived_sums = arrived_sums.reshape(steps, ep_count, tp_count, row_own, -1)
    summed = jnp.sum(arrived_sums, axis=2)
    projected = summed.astype(jnp.bfloat16)
    row_major = jnp.transpose(projected, (0, 2, 1, 3)).reshape(steps, row_own, width)

    residual = hidden_in.astype(jnp.float32) + row_major.astype(jnp.float32)
    mean_square = jnp.mean(residual * residual, axis=-1, keepdims=True)
    normed = (residual * lax.rsqrt(mean_square + norm_eps) * norm_gain).astype(jnp.bfloat16)
    weights = gate_scores / jnp.sum(gate_scores, axis=-1, keepdims=True)

    slots_per = steps * capacity
    expert_ids = routes.reshape(steps, -1)
    assigned = expert_ids.shape[1]
    matches = (
        expert_ids[:, :, None] == jnp.arange(expert_count, dtype=jnp.int32)[None, None, :]
    ).astype(jnp.int32)
    earlier = jnp.cumsum(matches, axis=1) - matches
    slot_rank = jnp.sum(earlier * matches, axis=2)
    step_ids = jnp.arange(steps, dtype=jnp.int32)[:, None]
    slot_index = (expert_ids * slots_per + step_ids * capacity + slot_rank).reshape(-1)
    slot_onehot = (
        slot_index[:, None] == jnp.arange(expert_count * slots_per, dtype=jnp.int32)[None, :]
    ).astype(jnp.bfloat16)
    row_ids = (step_ids * row_own + jnp.arange(assigned, dtype=jnp.int32)[None, :] // TOPK).reshape(-1)
    row_onehot = (
        row_ids[:, None] == jnp.arange(steps * row_own, dtype=jnp.int32)[None, :]
    ).astype(jnp.bfloat16)
    selector = jnp.einsum(
        "as,ar->sr", slot_onehot, row_onehot, preferred_element_type=jnp.float32
    ).astype(jnp.bfloat16)
    outgoing = jnp.dot(
        selector, normed.reshape(steps * row_own, width), preferred_element_type=jnp.float32
    ).astype(jnp.bfloat16)
    outgoing = outgoing.reshape(expert_count, slots_per, width)
    arrived = lax.all_to_all(outgoing, ("ep", "tp"), split_axis=0, concat_axis=0, tiled=True)
    flat_rows = arrived.reshape(-1, width)
    gate_act = jnp.dot(flat_rows, expert_gate[0], preferred_element_type=jnp.float32)
    up_act = jnp.dot(flat_rows, expert_up[0], preferred_element_type=jnp.float32)
    hidden = (jax.nn.silu(gate_act) * up_act).astype(jnp.bfloat16)
    expert_out = jnp.dot(hidden, expert_down[0], preferred_element_type=jnp.float32).astype(
        jnp.bfloat16
    )
    returned = lax.all_to_all(
        expert_out.reshape(arrived.shape), ("ep", "tp"), split_axis=0, concat_axis=0, tiled=True
    )
    returned = returned.reshape(expert_count * slots_per, width)
    selected = returned[slot_index].astype(jnp.float32) * weights.reshape(-1)[:, None]
    expert_mix = jnp.sum(selected.reshape(steps, row_own, TOPK, width), axis=2)
    return (residual + expert_mix).astype(jnp.bfloat16)


def solution(mesh):
    placed = (
        P(None, "ep", "tp"),
        P(None, None, "ep", "tp"),
        P(None, "ep", None, "tp"),
        P("ep"),
        P(None, ("ep", "tp"), None),
        P(),
        P("tp", "ep"),
        P(None, ("ep", "tp"), None),
        P(None, ("ep", "tp"), None),
        P(("ep", "tp"), None, None),
        P(("ep", "tp"), None, None),
        P(("ep", "tp"), None, None),
    )
    return jax.shard_map(
        per_device,
        mesh=mesh,
        in_specs=placed,
        out_specs=P(None, ("ep", "tp"), None),
        check_vma=False,
    )
```

```python
import jax
import jax.numpy as jnp
from jax import lax
from jax.sharding import PartitionSpec as P

HEAD_SIZE = 128
TOPK = 8
SLOTS = 256
DECODE_STEPS = 3


masked_score = -1e30
norm_eps = 1e-06


def per_device(
    query,
    step_key_value,
    key_value_cache,
    lengths,
    hidden_in,
    norm_gain,
    w_out,
    routes,
    gate_scores,
    expert_gate,
    expert_up,
    expert_down,
):
    ep_count = lax.axis_size("ep")
    tp_count = lax.axis_size("tp")
    steps = query.shape[0]
    row_dev = query.shape[1]
    row_own = hidden_in.shape[1]
    width = hidden_in.shape[2]
    heads_dev = query.shape[2] // HEAD_SIZE
    cache_len = key_value_cache.shape[2]
    expert_count = ep_count * tp_count * expert_gate.shape[0]
    capacity = SLOTS // expert_count
    score_scale = HEAD_SIZE ** (-0.5)
    stored_keys = key_value_cache[0]
    stored_values = key_value_cache[1]
    usable = jnp.arange(cache_len, dtype=jnp.int32)[None, :] < lengths[:, None]

    query_rows = query.reshape(steps, row_dev, heads_dev, HEAD_SIZE)
    incoming_keys = step_key_value[:, 0]
    incoming_values = step_key_value[:, 1]
    cache_scores = (
        jnp.einsum("srhd,rjd->srhj", query_rows, stored_keys, preferred_element_type=jnp.float32)
        * score_scale
    )
    cache_scores = jnp.where(usable[None, :, None, :], cache_scores, masked_score)
    fresh_scores = (
        jnp.einsum("srhd,jrd->srhj", query_rows, incoming_keys, preferred_element_type=jnp.float32)
        * score_scale
    )
    fresh_ok = (
        jnp.arange(steps, dtype=jnp.int32)[None, :] <= jnp.arange(steps, dtype=jnp.int32)[:, None]
    )
    fresh_scores = jnp.where(fresh_ok[:, None, None, :], fresh_scores, masked_score)
    scores = jnp.concatenate([cache_scores, fresh_scores], axis=-1)
    top = jnp.max(scores, axis=-1, keepdims=True)
    raised = jnp.exp(scores - top)
    probs = (raised / jnp.sum(raised, axis=-1, keepdims=True)).astype(jnp.bfloat16)
    attended = jnp.einsum(
        "srhj,rjd->srhd", probs[..., :cache_len], stored_values, preferred_element_type=jnp.float32
    )
    attended = attended + jnp.einsum(
        "srhj,jrd->srhd", probs[..., cache_len:], incoming_values, preferred_element_type=jnp.float32
    )
    attended = attended.astype(jnp.bfloat16).reshape(steps, row_dev, heads_dev * HEAD_SIZE)

    gathered = lax.all_gather(attended, "ep", axis=1, tiled=True)
    partial_sums = jnp.einsum(
        "srk,kc->src", gathered, w_out, preferred_element_type=jnp.float32
    )
    grouped = partial_sums.reshape(steps, ep_count * tp_count, row_own, -1)
    arrived_sums = lax.all_to_all(
        grouped, ("ep", "tp"), split_axis=1, concat_axis=1, tiled=True
    )
    arrived_sums = arrived_sums.reshape(steps, ep_count, tp_count, row_own, -1)
    summed = jnp.sum(arrived_sums, axis=2)
    projected = summed.astype(jnp.bfloat16)
    row_major = jnp.transpose(projected, (0, 2, 1, 3)).reshape(steps, row_own, width)

    residual = hidden_in.astype(jnp.float32) + row_major.astype(jnp.float32)
    mean_square = jnp.mean(residual * residual, axis=-1, keepdims=True)
    normed = (residual * lax.rsqrt(mean_square + norm_eps) * norm_gain).astype(jnp.bfloat16)
    weights = gate_scores / jnp.sum(gate_scores, axis=-1, keepdims=True)

    slots_per = steps * capacity
    expert_ids = routes.reshape(steps, -1)
    assigned = expert_ids.shape[1]
    matches = (
        expert_ids[:, :, None] == jnp.arange(expert_count, dtype=jnp.int32)[None, None, :]
    ).astype(jnp.int32)
    earlier = jnp.cumsum(matches, axis=1) - matches
    slot_rank = jnp.sum(earlier * matches, axis=2)
    step_ids = jnp.arange(steps, dtype=jnp.int32)[:, None]
    slot_index = (expert_ids * slots_per + step_ids * capacity + slot_rank).reshape(-1)
    slot_onehot = (
        slot_index[:, None] == jnp.arange(expert_count * slots_per, dtype=jnp.int32)[None, :]
    ).astype(jnp.bfloat16)
    row_ids = (step_ids * row_own + jnp.arange(assigned, dtype=jnp.int32)[None, :] // TOPK).reshape(-1)
    row_onehot = (
        row_ids[:, None] == jnp.arange(steps * row_own, dtype=jnp.int32)[None, :]
    ).astype(jnp.bfloat16)
    selector = jnp.einsum(
        "as,ar->sr", slot_onehot, row_onehot, preferred_element_type=jnp.float32
    ).astype(jnp.bfloat16)
    outgoing = jnp.dot(
        selector, normed.reshape(steps * row_own, width), preferred_element_type=jnp.float32
    ).astype(jnp.bfloat16)
    wire_shape = (expert_count, slots_per * width // 128, 128)
    outgoing = outgoing.reshape(wire_shape)
    arrived = lax.all_to_all(outgoing, ("ep", "tp"), split_axis=0, concat_axis=0, tiled=True)
    flat_rows = arrived.reshape(-1, width)
    gate_act = jnp.dot(flat_rows, expert_gate[0], preferred_element_type=jnp.float32)
    up_act = jnp.dot(flat_rows, expert_up[0], preferred_element_type=jnp.float32)
    hidden = (jax.nn.silu(gate_act) * up_act).astype(jnp.bfloat16)
    expert_out = jnp.dot(hidden, expert_down[0], preferred_element_type=jnp.float32).astype(
        jnp.bfloat16
    )
    returned = lax.all_to_all(
        expert_out.reshape(wire_shape), ("ep", "tp"), split_axis=0, concat_axis=0, tiled=True
    )
    returned = returned.reshape(expert_count * slots_per, width)
    selected = returned[slot_index].astype(jnp.float32) * weights.reshape(-1)[:, None]
    expert_mix = jnp.sum(selected.reshape(steps, row_own, TOPK, width), axis=2)
    return (residual + expert_mix).astype(jnp.bfloat16)


def solution(mesh):
    placed = (
        P(None, "ep", "tp"),
        P(None, None, "ep", "tp"),
        P(None, "ep", None, "tp"),
        P("ep"),
        P(None, ("ep", "tp"), None),
        P(),
        P("tp", "ep"),
        P(None, ("ep", "tp"), None),
        P(None, ("ep", "tp"), None),
        P(("ep", "tp"), None, None),
        P(("ep", "tp"), None, None),
        P(("ep", "tp"), None, None),
    )
    return jax.shard_map(
        per_device,
        mesh=mesh,
        in_specs=placed,
        out_specs=P(None, ("ep", "tp"), None),
        check_vma=False,
    )
```

```python
import jax
import jax.numpy as jnp
from jax import lax
from jax.sharding import Mesh, PartitionSpec as P

HEAD_SIZE = 128
TOPK = 8
SLOTS = 256
DECODE_STEPS = 3


masked_score = -1e30
norm_eps = 1e-06


def per_device(
    query,
    step_key_value,
    key_value_cache,
    lengths,
    hidden_in,
    norm_gain,
    w_out,
    routes,
    gate_scores,
    expert_gate,
    expert_up,
    expert_down,
):
    chip_count = lax.axis_size("eh")
    core_count = lax.axis_size("ec")
    ep_count = chip_count * core_count
    tp_count = lax.axis_size("tp")
    steps = query.shape[0]
    row_dev = query.shape[1]
    row_own = hidden_in.shape[1]
    width = hidden_in.shape[2]
    heads_dev = query.shape[2] // HEAD_SIZE
    cache_len = key_value_cache.shape[2]
    expert_count = ep_count * tp_count * expert_gate.shape[0]
    capacity = SLOTS // expert_count
    score_scale = HEAD_SIZE ** (-0.5)
    stored_keys = key_value_cache[0]
    stored_values = key_value_cache[1]
    usable = jnp.arange(cache_len, dtype=jnp.int32)[None, :] < lengths[:, None]

    query_rows = query.reshape(steps, row_dev, heads_dev, HEAD_SIZE)
    incoming_keys = step_key_value[:, 0]
    incoming_values = step_key_value[:, 1]
    cache_scores = (
        jnp.einsum("srhd,rjd->srhj", query_rows, stored_keys, preferred_element_type=jnp.float32)
        * score_scale
    )
    cache_scores = jnp.where(usable[None, :, None, :], cache_scores, masked_score)
    fresh_scores = (
        jnp.einsum("srhd,jrd->srhj", query_rows, incoming_keys, preferred_element_type=jnp.float32)
        * score_scale
    )
    fresh_ok = (
        jnp.arange(steps, dtype=jnp.int32)[None, :] <= jnp.arange(steps, dtype=jnp.int32)[:, None]
    )
    fresh_scores = jnp.where(fresh_ok[:, None, None, :], fresh_scores, masked_score)
    scores = jnp.concatenate([cache_scores, fresh_scores], axis=-1)
    top = jnp.max(scores, axis=-1, keepdims=True)
    raised = jnp.exp(scores - top)
    probs = (raised / jnp.sum(raised, axis=-1, keepdims=True)).astype(jnp.bfloat16)
    attended = jnp.einsum(
        "srhj,rjd->srhd", probs[..., :cache_len], stored_values, preferred_element_type=jnp.float32
    )
    attended = attended + jnp.einsum(
        "srhj,jrd->srhd", probs[..., cache_len:], incoming_values, preferred_element_type=jnp.float32
    )
    attended = attended.astype(jnp.bfloat16).reshape(steps, row_dev, heads_dev * HEAD_SIZE)

    w_pair = lax.all_gather(w_out, "ec", axis=1, tiled=True)
    gathered = lax.all_gather(attended, "eh", axis=1, tiled=True)
    partial_sums = jnp.einsum(
        "srk,kc->src", gathered, w_pair, preferred_element_type=jnp.float32
    )
    grouped = partial_sums.reshape(steps, chip_count * tp_count, row_own, -1)
    arrived_sums = lax.all_to_all(
        grouped, ("eh", "tp"), split_axis=1, concat_axis=1, tiled=True
    )
    arrived_sums = arrived_sums.reshape(steps, chip_count, tp_count, row_own, -1)
    summed = jnp.sum(arrived_sums, axis=2)
    projected = summed.astype(jnp.bfloat16)
    row_major = jnp.transpose(projected, (0, 2, 1, 3)).reshape(steps, row_own, width)

    residual = hidden_in.astype(jnp.float32) + row_major.astype(jnp.float32)
    mean_square = jnp.mean(residual * residual, axis=-1, keepdims=True)
    normed = (residual * lax.rsqrt(mean_square + norm_eps) * norm_gain).astype(jnp.bfloat16)
    weights = gate_scores / jnp.sum(gate_scores, axis=-1, keepdims=True)

    slots_per = steps * capacity
    expert_ids = routes.reshape(steps, -1)
    assigned = expert_ids.shape[1]
    matches = (
        expert_ids[:, :, None] == jnp.arange(expert_count, dtype=jnp.int32)[None, None, :]
    ).astype(jnp.int32)
    earlier = jnp.cumsum(matches, axis=1) - matches
    slot_rank = jnp.sum(earlier * matches, axis=2)
    step_ids = jnp.arange(steps, dtype=jnp.int32)[:, None]
    slot_index = (expert_ids * slots_per + step_ids * capacity + slot_rank).reshape(-1)
    slot_onehot = (
        slot_index[:, None] == jnp.arange(expert_count * slots_per, dtype=jnp.int32)[None, :]
    ).astype(jnp.bfloat16)
    row_ids = (step_ids * row_own + jnp.arange(assigned, dtype=jnp.int32)[None, :] // TOPK).reshape(-1)
    row_onehot = (
        row_ids[:, None] == jnp.arange(steps * row_own, dtype=jnp.int32)[None, :]
    ).astype(jnp.bfloat16)
    selector = jnp.einsum(
        "as,ar->sr", slot_onehot, row_onehot, preferred_element_type=jnp.float32
    ).astype(jnp.bfloat16)
    outgoing = jnp.dot(
        selector, normed.reshape(steps * row_own, width), preferred_element_type=jnp.float32
    ).astype(jnp.bfloat16)
    wire_shape = (expert_count, slots_per * width // 128, 128)
    outgoing = outgoing.reshape(wire_shape)
    arrived = lax.all_to_all(outgoing, ("eh", "ec", "tp"), split_axis=0, concat_axis=0, tiled=True)
    flat_rows = arrived.reshape(-1, width)
    gate_act = jnp.dot(flat_rows, expert_gate[0], preferred_element_type=jnp.float32)
    up_act = jnp.dot(flat_rows, expert_up[0], preferred_element_type=jnp.float32)
    hidden = (jax.nn.silu(gate_act) * up_act).astype(jnp.bfloat16)
    expert_out = jnp.dot(hidden, expert_down[0], preferred_element_type=jnp.float32).astype(
        jnp.bfloat16
    )
    returned = lax.all_to_all(
        expert_out.reshape(wire_shape), ("eh", "ec", "tp"), split_axis=0, concat_axis=0, tiled=True
    )
    returned = returned.reshape(expert_count * slots_per, width)
    selected = returned[slot_index].astype(jnp.float32) * weights.reshape(-1)[:, None]
    expert_mix = jnp.sum(selected.reshape(steps, row_own, TOPK, width), axis=2)
    return (residual + expert_mix).astype(jnp.bfloat16)


def solution(mesh):
    chips = mesh.devices.shape[0] // 2
    split_mesh = Mesh(
        mesh.devices.reshape(chips, 2, mesh.devices.shape[1]), ("eh", "ec", "tp")
    )
    ep = ("eh", "ec")
    placed = (
        P(None, ep, "tp"),
        P(None, None, ep, "tp"),
        P(None, ep, None, "tp"),
        P(ep),
        P(None, (*ep, "tp"), None),
        P(),
        P("tp", ep),
        P(None, (*ep, "tp"), None),
        P(None, (*ep, "tp"), None),
        P((*ep, "tp"), None, None),
        P((*ep, "tp"), None, None),
        P((*ep, "tp"), None, None),
    )
    return jax.shard_map(
        per_device,
        mesh=split_mesh,
        in_specs=placed,
        out_specs=P(None, (*ep, "tp"), None),
        check_vma=False,
    )
```

```python
import jax
import jax.numpy as jnp
from jax import lax
from jax.sharding import Mesh, PartitionSpec as P

HEAD_SIZE = 128
TOPK = 8
SLOTS = 256
DECODE_STEPS = 3


masked_score = -1e30
norm_eps = 1e-06


def per_device(
    query,
    step_key_value,
    key_value_cache,
    lengths,
    hidden_in,
    norm_gain,
    w_out,
    routes,
    gate_scores,
    expert_gate,
    expert_up,
    expert_down,
):
    chip_count = lax.axis_size("eh")
    core_count = lax.axis_size("ec")
    ep_count = chip_count * core_count
    tp_count = lax.axis_size("tp")
    steps = query.shape[0]
    row_dev = query.shape[1]
    row_own = hidden_in.shape[1]
    width = hidden_in.shape[2]
    heads_dev = query.shape[2] // HEAD_SIZE
    cache_len = key_value_cache.shape[2]
    expert_count = ep_count * tp_count * expert_gate.shape[0]
    capacity = SLOTS // expert_count
    score_scale = HEAD_SIZE ** (-0.5)
    stored_keys = key_value_cache[0]
    stored_values = key_value_cache[1]
    usable = jnp.arange(cache_len, dtype=jnp.int32)[None, :] < lengths[:, None]

    query_rows = query.reshape(steps, row_dev, heads_dev, HEAD_SIZE)
    incoming_keys = step_key_value[:, 0]
    incoming_values = step_key_value[:, 1]
    cache_scores = (
        jnp.einsum("srhd,rjd->srhj", query_rows, stored_keys, preferred_element_type=jnp.float32)
        * score_scale
    )
    cache_scores = jnp.where(usable[None, :, None, :], cache_scores, masked_score)
    fresh_scores = (
        jnp.einsum("srhd,jrd->srhj", query_rows, incoming_keys, preferred_element_type=jnp.float32)
        * score_scale
    )
    fresh_ok = (
        jnp.arange(steps, dtype=jnp.int32)[None, :] <= jnp.arange(steps, dtype=jnp.int32)[:, None]
    )
    fresh_scores = jnp.where(fresh_ok[:, None, None, :], fresh_scores, masked_score)
    scores = jnp.concatenate([cache_scores, fresh_scores], axis=-1)
    top = jnp.max(scores, axis=-1, keepdims=True)
    raised = jnp.exp(scores - top)
    probs = (raised / jnp.sum(raised, axis=-1, keepdims=True)).astype(jnp.bfloat16)
    attended = jnp.einsum(
        "srhj,rjd->srhd", probs[..., :cache_len], stored_values, preferred_element_type=jnp.float32
    )
    attended = attended + jnp.einsum(
        "srhj,jrd->srhd", probs[..., cache_len:], incoming_values, preferred_element_type=jnp.float32
    )
    attended = attended.astype(jnp.bfloat16).reshape(steps, row_dev, heads_dev * HEAD_SIZE)

    w_pair = lax.all_gather(w_out, "ec", axis=1, tiled=True)
    blocks = width // 128
    wire_shape = (expert_count, capacity * blocks, 128)
    results = []
    for step in range(steps):
        gathered = lax.all_gather(attended[step], "eh", axis=0, tiled=True)
        partial_sums = jnp.dot(gathered, w_pair, preferred_element_type=jnp.float32)
        grouped = partial_sums.reshape(chip_count * tp_count, row_own, -1)
        arrived_sums = lax.all_to_all(
            grouped, ("eh", "tp"), split_axis=0, concat_axis=0, tiled=True
        )
        arrived_sums = arrived_sums.reshape(chip_count, tp_count, row_own, -1)
        projected = jnp.sum(arrived_sums, axis=1).astype(jnp.bfloat16)
        row_major = jnp.transpose(projected, (1, 0, 2)).reshape(row_own, width)

        residual = hidden_in[step].astype(jnp.float32) + row_major.astype(jnp.float32)
        mean_square = jnp.mean(residual * residual, axis=-1, keepdims=True)
        normed = (residual * lax.rsqrt(mean_square + norm_eps) * norm_gain).astype(jnp.bfloat16)
        weights = gate_scores[step] / jnp.sum(gate_scores[step], axis=-1, keepdims=True)

        expert_ids = routes[step].reshape(-1)
        assigned = expert_ids.shape[0]
        matches = (
            expert_ids[:, None] == jnp.arange(expert_count, dtype=jnp.int32)[None, :]
        ).astype(jnp.int32)
        earlier = jnp.cumsum(matches, axis=0) - matches
        slot_rank = jnp.sum(earlier * matches, axis=1)
        slot_index = expert_ids * capacity + slot_rank
        slot_onehot = (
            slot_index[:, None] == jnp.arange(expert_count * capacity, dtype=jnp.int32)[None, :]
        ).astype(jnp.bfloat16)
        row_onehot = (
            (jnp.arange(assigned, dtype=jnp.int32) // TOPK)[:, None]
            == jnp.arange(row_own, dtype=jnp.int32)[None, :]
        ).astype(jnp.bfloat16)
        selector = jnp.einsum(
            "as,ar->sr", slot_onehot, row_onehot, preferred_element_type=jnp.float32
        ).astype(jnp.bfloat16)
        outgoing = jnp.dot(selector, normed, preferred_element_type=jnp.float32).astype(
            jnp.bfloat16
        )
        arrived = lax.all_to_all(
            outgoing.reshape(wire_shape), ("eh", "ec", "tp"), split_axis=0, concat_axis=0,
            tiled=True,
        )
        flat_rows = arrived.reshape(-1, width)
        gate_act = jnp.dot(flat_rows, expert_gate[0], preferred_element_type=jnp.float32)
        up_act = jnp.dot(flat_rows, expert_up[0], preferred_element_type=jnp.float32)
        hidden = (jax.nn.silu(gate_act) * up_act).astype(jnp.bfloat16)
        expert_out = jnp.dot(hidden, expert_down[0], preferred_element_type=jnp.float32).astype(
            jnp.bfloat16
        )
        returned = lax.all_to_all(
            expert_out.reshape(wire_shape), ("eh", "ec", "tp"), split_axis=0, concat_axis=0,
            tiled=True,
        )
        returned = returned.reshape(expert_count * capacity, width)
        selected = returned[slot_index].astype(jnp.float32) * weights.reshape(-1)[:, None]
        expert_mix = jnp.sum(selected.reshape(row_own, TOPK, width), axis=1)
        results.append((residual + expert_mix).astype(jnp.bfloat16))
    return jnp.stack(results)


def solution(mesh):
    chips = mesh.devices.shape[0] // 2
    split_mesh = Mesh(
        mesh.devices.reshape(chips, 2, mesh.devices.shape[1]), ("eh", "ec", "tp")
    )
    ep = ("eh", "ec")
    placed = (
        P(None, ep, "tp"),
        P(None, None, ep, "tp"),
        P(None, ep, None, "tp"),
        P(ep),
        P(None, (*ep, "tp"), None),
        P(),
        P("tp", ep),
        P(None, (*ep, "tp"), None),
        P(None, (*ep, "tp"), None),
        P((*ep, "tp"), None, None),
        P((*ep, "tp"), None, None),
        P((*ep, "tp"), None, None),
    )
    return jax.shard_map(
        per_device,
        mesh=split_mesh,
        in_specs=placed,
        out_specs=P(None, (*ep, "tp"), None),
        check_vma=False,
    )
```

```python
import jax
import jax.numpy as jnp
from jax import lax
from jax.sharding import PartitionSpec as P

HEAD_SIZE = 128
TOPK = 8
SLOTS = 256
DECODE_STEPS = 3


masked_score = -1e30
norm_eps = 1e-06


def per_device(
    query,
    step_key_value,
    key_value_cache,
    lengths,
    hidden_in,
    norm_gain,
    w_out,
    routes,
    gate_scores,
    expert_gate,
    expert_up,
    expert_down,
):
    ep_count = lax.axis_size("ep")
    tp_count = lax.axis_size("tp")
    steps = query.shape[0]
    row_dev = query.shape[1]
    row_own = hidden_in.shape[1]
    width = hidden_in.shape[2]
    heads_dev = query.shape[2] // HEAD_SIZE
    cache_len = key_value_cache.shape[2]
    expert_count = ep_count * tp_count * expert_gate.shape[0]
    capacity = SLOTS // expert_count
    score_scale = HEAD_SIZE ** (-0.5)
    stored_keys = key_value_cache[0]
    stored_values = key_value_cache[1]
    usable = jnp.arange(cache_len, dtype=jnp.int32)[None, :] < lengths[:, None]

    query_rows = query.reshape(steps, row_dev, heads_dev, HEAD_SIZE)
    incoming_keys = step_key_value[:, 0]
    incoming_values = step_key_value[:, 1]
    cache_scores = (
        jnp.einsum("srhd,rjd->srhj", query_rows, stored_keys, preferred_element_type=jnp.float32)
        * score_scale
    )
    cache_scores = jnp.where(usable[None, :, None, :], cache_scores, masked_score)
    fresh_scores = (
        jnp.einsum("srhd,jrd->srhj", query_rows, incoming_keys, preferred_element_type=jnp.float32)
        * score_scale
    )
    fresh_ok = (
        jnp.arange(steps, dtype=jnp.int32)[None, :] <= jnp.arange(steps, dtype=jnp.int32)[:, None]
    )
    fresh_scores = jnp.where(fresh_ok[:, None, None, :], fresh_scores, masked_score)
    scores = jnp.concatenate([cache_scores, fresh_scores], axis=-1)
    top = jnp.max(scores, axis=-1, keepdims=True)
    raised = jnp.exp(scores - top)
    probs = (raised / jnp.sum(raised, axis=-1, keepdims=True)).astype(jnp.bfloat16)
    attended = jnp.einsum(
        "srhj,rjd->srhd", probs[..., :cache_len], stored_values, preferred_element_type=jnp.float32
    )
    attended = attended + jnp.einsum(
        "srhj,jrd->srhd", probs[..., cache_len:], incoming_values, preferred_element_type=jnp.float32
    )
    attended = attended.astype(jnp.bfloat16).reshape(steps, row_dev, heads_dev * HEAD_SIZE)

    gathered = lax.all_gather(attended, "ep", axis=1, tiled=True)
    partial_sums = jnp.einsum(
        "srk,kc->src", gathered, w_out, preferred_element_type=jnp.float32
    )
    grouped = partial_sums.reshape(steps, ep_count * tp_count, row_own, -1)
    arrived_sums = lax.all_to_all(
        grouped, ("ep", "tp"), split_axis=1, concat_axis=1, tiled=True
    )
    arrived_sums = arrived_sums.reshape(steps, ep_count, tp_count, row_own, -1)
    summed = jnp.sum(arrived_sums, axis=2)
    projected = summed.astype(jnp.bfloat16)
    row_major = jnp.transpose(projected, (0, 2, 1, 3)).reshape(steps, row_own, width)

    residual = hidden_in.astype(jnp.float32) + row_major.astype(jnp.float32)
    mean_square = jnp.mean(residual * residual, axis=-1, keepdims=True)
    normed = (residual * lax.rsqrt(mean_square + norm_eps) * norm_gain).astype(jnp.bfloat16)
    weights = gate_scores / jnp.sum(gate_scores, axis=-1, keepdims=True)

    slots_per = steps * capacity
    expert_ids = routes.reshape(steps, -1)
    assigned = expert_ids.shape[1]
    matches = (
        expert_ids[:, :, None] == jnp.arange(expert_count, dtype=jnp.int32)[None, None, :]
    ).astype(jnp.int32)
    earlier = jnp.cumsum(matches, axis=1) - matches
    slot_rank = jnp.sum(earlier * matches, axis=2)
    step_ids = jnp.arange(steps, dtype=jnp.int32)[:, None]
    slot_index = (expert_ids * slots_per + step_ids * capacity + slot_rank).reshape(-1)
    row_ids = (step_ids * row_own + jnp.arange(assigned, dtype=jnp.int32)[None, :] // TOPK).reshape(-1)
    empty = steps * row_own
    source_row = jnp.full((expert_count * slots_per,), empty, jnp.int32).at[slot_index].set(row_ids)
    blocks = width // 128
    padded = jnp.concatenate(
        [normed.reshape(steps * row_own, blocks, 128), jnp.zeros((1, blocks, 128), jnp.bfloat16)]
    )
    wire_shape = (expert_count, slots_per * blocks, 128)
    outgoing = jnp.take(padded, source_row, axis=0).reshape(wire_shape)
    arrived = lax.all_to_all(outgoing, ("ep", "tp"), split_axis=0, concat_axis=0, tiled=True)
    flat_rows = arrived.reshape(-1, width)
    gate_act = jnp.dot(flat_rows, expert_gate[0], preferred_element_type=jnp.float32)
    up_act = jnp.dot(flat_rows, expert_up[0], preferred_element_type=jnp.float32)
    hidden = (jax.nn.silu(gate_act) * up_act).astype(jnp.bfloat16)
    expert_out = jnp.dot(hidden, expert_down[0], preferred_element_type=jnp.float32).astype(
        jnp.bfloat16
    )
    returned = lax.all_to_all(
        expert_out.reshape(wire_shape), ("ep", "tp"), split_axis=0, concat_axis=0, tiled=True
    )
    returned = returned.reshape(expert_count * slots_per, blocks, 128)
    selected = jnp.take(returned, slot_index, axis=0).astype(jnp.float32)
    selected = selected * weights.reshape(-1)[:, None, None]
    expert_mix = jnp.sum(selected.reshape(steps, row_own, TOPK, blocks, 128), axis=2)
    expert_mix = expert_mix.reshape(steps, row_own, width)
    return (residual + expert_mix).astype(jnp.bfloat16)


def solution(mesh):
    placed = (
        P(None, "ep", "tp"),
        P(None, None, "ep", "tp"),
        P(None, "ep", None, "tp"),
        P("ep"),
        P(None, ("ep", "tp"), None),
        P(),
        P("tp", "ep"),
        P(None, ("ep", "tp"), None),
        P(None, ("ep", "tp"), None),
        P(("ep", "tp"), None, None),
        P(("ep", "tp"), None, None),
        P(("ep", "tp"), None, None),
    )
    return jax.shard_map(
        per_device,
        mesh=mesh,
        in_specs=placed,
        out_specs=P(None, ("ep", "tp"), None),
        check_vma=False,
    )
```

```python
import jax
import jax.numpy as jnp
from jax import lax
from jax.sharding import Mesh, PartitionSpec as P

HEAD_SIZE = 128
TOPK = 8
SLOTS = 256
DECODE_STEPS = 3


masked_score = -1e30
norm_eps = 1e-06


def per_device(
    query,
    step_key_value,
    key_value_cache,
    lengths,
    hidden_in,
    norm_gain,
    w_out,
    routes,
    gate_scores,
    expert_gate,
    expert_up,
    expert_down,
):
    x_count = lax.axis_size("x")
    yc_count = lax.axis_size("y") * lax.axis_size("c")
    ep_count = x_count * yc_count
    tp_count = lax.axis_size("tp")
    steps = query.shape[0]
    row_dev = query.shape[1]
    row_own = hidden_in.shape[1]
    width = hidden_in.shape[2]
    heads_dev = query.shape[2] // HEAD_SIZE
    cache_len = key_value_cache.shape[2]
    expert_count = ep_count * tp_count * expert_gate.shape[0]
    capacity = SLOTS // expert_count
    score_scale = HEAD_SIZE ** (-0.5)
    stored_keys = key_value_cache[0]
    stored_values = key_value_cache[1]
    usable = jnp.arange(cache_len, dtype=jnp.int32)[None, :] < lengths[:, None]

    query_rows = query.reshape(steps, row_dev, heads_dev, HEAD_SIZE)
    incoming_keys = step_key_value[:, 0]
    incoming_values = step_key_value[:, 1]
    cache_scores = (
        jnp.einsum("srhd,rjd->srhj", query_rows, stored_keys, preferred_element_type=jnp.float32)
        * score_scale
    )
    cache_scores = jnp.where(usable[None, :, None, :], cache_scores, masked_score)
    fresh_scores = (
        jnp.einsum("srhd,jrd->srhj", query_rows, incoming_keys, preferred_element_type=jnp.float32)
        * score_scale
    )
    fresh_ok = (
        jnp.arange(steps, dtype=jnp.int32)[None, :] <= jnp.arange(steps, dtype=jnp.int32)[:, None]
    )
    fresh_scores = jnp.where(fresh_ok[:, None, None, :], fresh_scores, masked_score)
    scores = jnp.concatenate([cache_scores, fresh_scores], axis=-1)
    top = jnp.max(scores, axis=-1, keepdims=True)
    raised = jnp.exp(scores - top)
    probs = (raised / jnp.sum(raised, axis=-1, keepdims=True)).astype(jnp.bfloat16)
    attended = jnp.einsum(
        "srhj,rjd->srhd", probs[..., :cache_len], stored_values, preferred_element_type=jnp.float32
    )
    attended = attended + jnp.einsum(
        "srhj,jrd->srhd", probs[..., cache_len:], incoming_values, preferred_element_type=jnp.float32
    )
    attended = attended.astype(jnp.bfloat16).reshape(steps, row_dev, heads_dev * HEAD_SIZE)

    w_cols = lax.all_gather(w_out, "x", axis=1, tiled=True)
    gathered = lax.all_gather(attended, ("y", "c"), axis=1, tiled=True)
    partial_sums = jnp.einsum(
        "srk,kc->src", gathered, w_cols, preferred_element_type=jnp.float32
    )
    grouped = partial_sums.reshape(steps, yc_count * tp_count, row_own, -1)
    arrived_sums = lax.all_to_all(
        grouped, ("y", "c", "tp"), split_axis=1, concat_axis=1, tiled=True
    )
    arrived_sums = arrived_sums.reshape(steps, yc_count, tp_count, row_own, x_count, -1)
    summed = jnp.sum(arrived_sums, axis=2)
    projected = summed.astype(jnp.bfloat16)
    row_major = jnp.transpose(projected, (0, 2, 3, 1, 4)).reshape(steps, row_own, width)

    residual = hidden_in.astype(jnp.float32) + row_major.astype(jnp.float32)
    mean_square = jnp.mean(residual * residual, axis=-1, keepdims=True)
    normed = (residual * lax.rsqrt(mean_square + norm_eps) * norm_gain).astype(jnp.bfloat16)
    weights = gate_scores / jnp.sum(gate_scores, axis=-1, keepdims=True)

    slots_per = steps * capacity
    expert_ids = routes.reshape(steps, -1)
    assigned = expert_ids.shape[1]
    matches = (
        expert_ids[:, :, None] == jnp.arange(expert_count, dtype=jnp.int32)[None, None, :]
    ).astype(jnp.int32)
    earlier = jnp.cumsum(matches, axis=1) - matches
    slot_rank = jnp.sum(earlier * matches, axis=2)
    step_ids = jnp.arange(steps, dtype=jnp.int32)[:, None]
    slot_index = (expert_ids * slots_per + step_ids * capacity + slot_rank).reshape(-1)
    row_ids = (step_ids * row_own + jnp.arange(assigned, dtype=jnp.int32)[None, :] // TOPK).reshape(-1)
    empty = steps * row_own
    source_row = jnp.full((expert_count * slots_per,), empty, jnp.int32).at[slot_index].set(row_ids)
    blocks = width // 128
    padded = jnp.concatenate(
        [normed.reshape(steps * row_own, blocks, 128), jnp.zeros((1, blocks, 128), jnp.bfloat16)]
    )
    wire_shape = (expert_count, slots_per * blocks, 128)
    outgoing = jnp.take(padded, source_row, axis=0).reshape(wire_shape)
    arrived = lax.all_to_all(outgoing, ("x", "y", "c", "tp"), split_axis=0, concat_axis=0, tiled=True)
    flat_rows = arrived.reshape(-1, width)
    gate_act = jnp.dot(flat_rows, expert_gate[0], preferred_element_type=jnp.float32)
    up_act = jnp.dot(flat_rows, expert_up[0], preferred_element_type=jnp.float32)
    hidden = (jax.nn.silu(gate_act) * up_act).astype(jnp.bfloat16)
    expert_out = jnp.dot(hidden, expert_down[0], preferred_element_type=jnp.float32).astype(
        jnp.bfloat16
    )
    returned = lax.all_to_all(
        expert_out.reshape(wire_shape), ("x", "y", "c", "tp"), split_axis=0, concat_axis=0, tiled=True
    )
    returned = returned.reshape(expert_count * slots_per, blocks, 128)
    selected = jnp.take(returned, slot_index, axis=0).astype(jnp.float32)
    selected = selected * weights.reshape(-1)[:, None, None]
    expert_mix = jnp.sum(selected.reshape(steps, row_own, TOPK, blocks, 128), axis=2)
    expert_mix = expert_mix.reshape(steps, row_own, width)
    return (residual + expert_mix).astype(jnp.bfloat16)


def solution(mesh):
    ep_size, tp_size = mesh.devices.shape
    x_size = ep_size // 8
    split_mesh = Mesh(
        mesh.devices.reshape(x_size, ep_size // (2 * x_size), 2, tp_size), ("x", "y", "c", "tp")
    )
    ep = ("x", "y", "c")
    placed = (
        P(None, ep, "tp"),
        P(None, None, ep, "tp"),
        P(None, ep, None, "tp"),
        P(ep),
        P(None, (*ep, "tp"), None),
        P(),
        P("tp", ep),
        P(None, (*ep, "tp"), None),
        P(None, (*ep, "tp"), None),
        P((*ep, "tp"), None, None),
        P((*ep, "tp"), None, None),
        P((*ep, "tp"), None, None),
    )
    return jax.shard_map(
        per_device,
        mesh=split_mesh,
        in_specs=placed,
        out_specs=P(None, (*ep, "tp"), None),
        check_vma=False,
    )
```

```python
import jax
import jax.numpy as jnp
from jax import lax
from jax.sharding import Mesh, PartitionSpec as P

HEAD_SIZE = 128
TOPK = 8
SLOTS = 256
DECODE_STEPS = 3


masked_score = -1e30
norm_eps = 1e-06


def per_device(
    query,
    step_key_value,
    key_value_cache,
    lengths,
    hidden_in,
    norm_gain,
    w_out,
    routes,
    gate_scores,
    expert_gate,
    expert_up,
    expert_down,
):
    x_count = lax.axis_size("x")
    yc_count = lax.axis_size("y") * lax.axis_size("c")
    ep_count = x_count * yc_count
    tp_count = lax.axis_size("tp")
    steps = query.shape[0]
    row_dev = query.shape[1]
    row_own = hidden_in.shape[1]
    width = hidden_in.shape[2]
    heads_dev = query.shape[2] // HEAD_SIZE
    cache_len = key_value_cache.shape[2]
    expert_count = ep_count * tp_count * expert_gate.shape[0]
    capacity = SLOTS // expert_count
    score_scale = HEAD_SIZE ** (-0.5)
    stored_keys = key_value_cache[0]
    stored_values = key_value_cache[1]
    usable = jnp.arange(cache_len, dtype=jnp.int32)[None, :] < lengths[:, None]

    query_rows = query.reshape(steps, row_dev, heads_dev, HEAD_SIZE)
    incoming_keys = step_key_value[:, 0]
    incoming_values = step_key_value[:, 1]
    cache_scores = (
        jnp.einsum("srhd,rjd->srhj", query_rows, stored_keys, preferred_element_type=jnp.float32)
        * score_scale
    )
    cache_scores = jnp.where(usable[None, :, None, :], cache_scores, masked_score)
    fresh_scores = (
        jnp.einsum("srhd,jrd->srhj", query_rows, incoming_keys, preferred_element_type=jnp.float32)
        * score_scale
    )
    fresh_ok = (
        jnp.arange(steps, dtype=jnp.int32)[None, :] <= jnp.arange(steps, dtype=jnp.int32)[:, None]
    )
    fresh_scores = jnp.where(fresh_ok[:, None, None, :], fresh_scores, masked_score)
    scores = jnp.concatenate([cache_scores, fresh_scores], axis=-1)
    top = jnp.max(scores, axis=-1, keepdims=True)
    raised = jnp.exp(scores - top)
    probs = (raised / jnp.sum(raised, axis=-1, keepdims=True)).astype(jnp.bfloat16)
    attended = jnp.einsum(
        "srhj,rjd->srhd", probs[..., :cache_len], stored_values, preferred_element_type=jnp.float32
    )
    attended = attended + jnp.einsum(
        "srhj,jrd->srhd", probs[..., cache_len:], incoming_values, preferred_element_type=jnp.float32
    )
    attended = attended.astype(jnp.bfloat16).reshape(steps, row_dev, heads_dev * HEAD_SIZE)

    x_here = lax.axis_index("x")
    shifted = [w_out] + [
        lax.ppermute(w_out, "x", [(i, (i + k) % x_count) for i in range(x_count)])
        for k in range(1, x_count)
    ]
    order = (x_here - jnp.arange(x_count, dtype=jnp.int32)) % x_count
    w_cols = jnp.take(jnp.stack(shifted), order, axis=0)
    w_cols = jnp.transpose(w_cols, (1, 0, 2)).reshape(w_out.shape[0], -1)
    gathered = lax.all_gather(attended, ("y", "c"), axis=1, tiled=True)
    partial_sums = jnp.einsum(
        "srk,kc->src", gathered, w_cols, preferred_element_type=jnp.float32
    )
    grouped = partial_sums.reshape(steps, yc_count * tp_count, row_own, -1)
    arrived_sums = lax.all_to_all(
        grouped, ("y", "c", "tp"), split_axis=1, concat_axis=1, tiled=True
    )
    arrived_sums = arrived_sums.reshape(steps, yc_count, tp_count, row_own, x_count, -1)
    summed = jnp.sum(arrived_sums, axis=2)
    projected = summed.astype(jnp.bfloat16)
    row_major = jnp.transpose(projected, (0, 2, 3, 1, 4)).reshape(steps, row_own, width)

    residual = hidden_in.astype(jnp.float32) + row_major.astype(jnp.float32)
    mean_square = jnp.mean(residual * residual, axis=-1, keepdims=True)
    normed = (residual * lax.rsqrt(mean_square + norm_eps) * norm_gain).astype(jnp.bfloat16)
    weights = gate_scores / jnp.sum(gate_scores, axis=-1, keepdims=True)

    slots_per = steps * capacity
    expert_ids = routes.reshape(steps, -1)
    assigned = expert_ids.shape[1]
    matches = (
        expert_ids[:, :, None] == jnp.arange(expert_count, dtype=jnp.int32)[None, None, :]
    ).astype(jnp.int32)
    earlier = jnp.cumsum(matches, axis=1) - matches
    slot_rank = jnp.sum(earlier * matches, axis=2)
    step_ids = jnp.arange(steps, dtype=jnp.int32)[:, None]
    slot_index = (expert_ids * slots_per + step_ids * capacity + slot_rank).reshape(-1)
    row_ids = (step_ids * row_own + jnp.arange(assigned, dtype=jnp.int32)[None, :] // TOPK).reshape(-1)
    empty = steps * row_own
    source_row = jnp.full((expert_count * slots_per,), empty, jnp.int32).at[slot_index].set(row_ids)
    blocks = width // 128
    padded = jnp.concatenate(
        [normed.reshape(steps * row_own, blocks, 128), jnp.zeros((1, blocks, 128), jnp.bfloat16)]
    )
    wire_shape = (expert_count, slots_per * blocks, 128)
    outgoing = jnp.take(padded, source_row, axis=0).reshape(wire_shape)
    arrived = lax.all_to_all(outgoing, ("x", "y", "c", "tp"), split_axis=0, concat_axis=0, tiled=True)
    flat_rows = arrived.reshape(-1, width)
    gate_act = jnp.dot(flat_rows, expert_gate[0], preferred_element_type=jnp.float32)
    up_act = jnp.dot(flat_rows, expert_up[0], preferred_element_type=jnp.float32)
    hidden = (jax.nn.silu(gate_act) * up_act).astype(jnp.bfloat16)
    expert_out = jnp.dot(hidden, expert_down[0], preferred_element_type=jnp.float32).astype(
        jnp.bfloat16
    )
    returned = lax.all_to_all(
        expert_out.reshape(wire_shape), ("x", "y", "c", "tp"), split_axis=0, concat_axis=0, tiled=True
    )
    returned = returned.reshape(expert_count * slots_per, blocks, 128)
    selected = jnp.take(returned, slot_index, axis=0).astype(jnp.float32)
    selected = selected * weights.reshape(-1)[:, None, None]
    expert_mix = jnp.sum(selected.reshape(steps, row_own, TOPK, blocks, 128), axis=2)
    expert_mix = expert_mix.reshape(steps, row_own, width)
    return (residual + expert_mix).astype(jnp.bfloat16)


def solution(mesh):
    ep_size, tp_size = mesh.devices.shape
    x_size = ep_size // 8
    split_mesh = Mesh(
        mesh.devices.reshape(x_size, ep_size // (2 * x_size), 2, tp_size), ("x", "y", "c", "tp")
    )
    ep = ("x", "y", "c")
    placed = (
        P(None, ep, "tp"),
        P(None, None, ep, "tp"),
        P(None, ep, None, "tp"),
        P(ep),
        P(None, (*ep, "tp"), None),
        P(),
        P("tp", ep),
        P(None, (*ep, "tp"), None),
        P(None, (*ep, "tp"), None),
        P((*ep, "tp"), None, None),
        P((*ep, "tp"), None, None),
        P((*ep, "tp"), None, None),
    )
    return jax.shard_map(
        per_device,
        mesh=split_mesh,
        in_specs=placed,
        out_specs=P(None, (*ep, "tp"), None),
        check_vma=False,
    )
```

```python
import jax
import jax.numpy as jnp
from jax import lax
from jax.sharding import Mesh, PartitionSpec as P

HEAD_SIZE = 128
TOPK = 8
SLOTS = 256
DECODE_STEPS = 3


masked_score = -1e30
norm_eps = 1e-06


def per_device(
    query,
    step_key_value,
    key_value_cache,
    lengths,
    hidden_in,
    norm_gain,
    w_out,
    routes,
    gate_scores,
    expert_gate,
    expert_up,
    expert_down,
):
    x_count = lax.axis_size("x")
    yc_count = lax.axis_size("y") * lax.axis_size("c")
    ep_count = x_count * yc_count
    tp_count = lax.axis_size("tp")
    steps = query.shape[0]
    row_dev = query.shape[1]
    row_own = hidden_in.shape[1]
    width = hidden_in.shape[2]
    heads_dev = query.shape[2] // HEAD_SIZE
    cache_len = key_value_cache.shape[2]
    expert_count = ep_count * tp_count * expert_gate.shape[0]
    capacity = SLOTS // expert_count
    score_scale = HEAD_SIZE ** (-0.5)
    stored_keys = key_value_cache[0]
    stored_values = key_value_cache[1]
    usable = jnp.arange(cache_len, dtype=jnp.int32)[None, :] < lengths[:, None]

    query_rows = query.reshape(steps, row_dev, heads_dev, HEAD_SIZE)
    incoming_keys = step_key_value[:, 0]
    incoming_values = step_key_value[:, 1]
    cache_scores = (
        jnp.einsum("srhd,rjd->srhj", query_rows, stored_keys, preferred_element_type=jnp.float32)
        * score_scale
    )
    cache_scores = jnp.where(usable[None, :, None, :], cache_scores, masked_score)
    fresh_scores = (
        jnp.einsum("srhd,jrd->srhj", query_rows, incoming_keys, preferred_element_type=jnp.float32)
        * score_scale
    )
    fresh_ok = (
        jnp.arange(steps, dtype=jnp.int32)[None, :] <= jnp.arange(steps, dtype=jnp.int32)[:, None]
    )
    fresh_scores = jnp.where(fresh_ok[:, None, None, :], fresh_scores, masked_score)
    scores = jnp.concatenate([cache_scores, fresh_scores], axis=-1)
    top = jnp.max(scores, axis=-1, keepdims=True)
    raised = jnp.exp(scores - top)
    probs = (raised / jnp.sum(raised, axis=-1, keepdims=True)).astype(jnp.bfloat16)
    attended = jnp.einsum(
        "srhj,rjd->srhd", probs[..., :cache_len], stored_values, preferred_element_type=jnp.float32
    )
    attended = attended + jnp.einsum(
        "srhj,jrd->srhd", probs[..., cache_len:], incoming_values, preferred_element_type=jnp.float32
    )
    attended = attended.astype(jnp.bfloat16).reshape(steps, row_dev, heads_dev * HEAD_SIZE)

    x_here = lax.axis_index("x")
    shifted = [w_out] + [
        lax.ppermute(w_out, "x", [(i, (i + k) % x_count) for i in range(x_count)])
        for k in range(1, x_count)
    ]
    order = (x_here - jnp.arange(x_count, dtype=jnp.int32)) % x_count
    w_cols = jnp.take(jnp.stack(shifted), order, axis=0, mode="clip")
    w_cols = jnp.transpose(w_cols, (1, 0, 2)).reshape(w_out.shape[0], -1)
    gathered = lax.all_gather(attended, ("y", "c"), axis=1, tiled=True)
    partial_sums = jnp.einsum(
        "srk,kc->src", gathered, w_cols, preferred_element_type=jnp.float32
    )
    grouped = partial_sums.reshape(steps, yc_count * tp_count, row_own, -1)
    arrived_sums = lax.all_to_all(
        grouped, ("y", "c", "tp"), split_axis=1, concat_axis=1, tiled=True
    )
    arrived_sums = arrived_sums.reshape(steps, yc_count, tp_count, row_own, x_count, -1)
    summed = jnp.sum(arrived_sums, axis=2)
    projected = summed.astype(jnp.bfloat16)
    row_major = jnp.transpose(projected, (0, 2, 3, 1, 4)).reshape(steps, row_own, width)

    residual = hidden_in.astype(jnp.float32) + row_major.astype(jnp.float32)
    mean_square = jnp.mean(residual * residual, axis=-1, keepdims=True)
    normed = (residual * lax.rsqrt(mean_square + norm_eps) * norm_gain).astype(jnp.bfloat16)
    weights = gate_scores / jnp.sum(gate_scores, axis=-1, keepdims=True)

    slots_per = steps * capacity
    expert_ids = routes.reshape(steps, -1)
    assigned = expert_ids.shape[1]
    matches = (
        expert_ids[:, :, None] == jnp.arange(expert_count, dtype=jnp.int32)[None, None, :]
    ).astype(jnp.int32)
    earlier = jnp.cumsum(matches, axis=1) - matches
    slot_rank = jnp.sum(earlier * matches, axis=2)
    step_ids = jnp.arange(steps, dtype=jnp.int32)[:, None]
    slot_index = (expert_ids * slots_per + step_ids * capacity + slot_rank).reshape(-1)
    row_ids = (step_ids * row_own + jnp.arange(assigned, dtype=jnp.int32)[None, :] // TOPK).reshape(-1)
    empty = steps * row_own
    source_row = jnp.full((expert_count * slots_per,), empty, jnp.int32).at[slot_index].set(row_ids)
    blocks = width // 128
    padded = jnp.concatenate(
        [normed.reshape(steps * row_own, blocks, 128), jnp.zeros((1, blocks, 128), jnp.bfloat16)]
    )
    source_by_step = source_row.reshape(expert_count, steps, capacity)
    chunks = ((0, steps - 1), (steps - 1, steps)) if steps > 1 else ((0, steps),)
    group = ("x", "y", "c", "tp")
    picked = []
    for first, last in chunks:
        span = (last - first) * capacity
        wire_shape = (expert_count, span * blocks, 128)
        chunk_rows = source_by_step[:, first:last].reshape(-1)
        outgoing = jnp.take(padded, chunk_rows, axis=0, mode="clip").reshape(wire_shape)
        arrived = lax.all_to_all(outgoing, group, split_axis=0, concat_axis=0, tiled=True)
        flat_rows = arrived.reshape(-1, width)
        gate_act = jnp.dot(flat_rows, expert_gate[0], preferred_element_type=jnp.float32)
        up_act = jnp.dot(flat_rows, expert_up[0], preferred_element_type=jnp.float32)
        hidden = (jax.nn.silu(gate_act) * up_act).astype(jnp.bfloat16)
        expert_out = jnp.dot(
            hidden, expert_down[0], preferred_element_type=jnp.float32
        ).astype(jnp.bfloat16)
        returned = lax.all_to_all(
            expert_out.reshape(wire_shape), group, split_axis=0, concat_axis=0, tiled=True
        )
        returned = returned.reshape(expert_count * span, blocks, 128)
        local_slot = (
            expert_ids[first:last] * span
            + (step_ids[first:last] - first) * capacity
            + slot_rank[first:last]
        ).reshape(-1)
        picked.append(jnp.take(returned, local_slot, axis=0, mode="clip"))
    selected = jnp.concatenate(picked).astype(jnp.float32)
    selected = selected * weights.reshape(-1)[:, None, None]
    expert_mix = jnp.sum(selected.reshape(steps, row_own, TOPK, blocks, 128), axis=2)
    expert_mix = expert_mix.reshape(steps, row_own, width)
    return (residual + expert_mix).astype(jnp.bfloat16)


def solution(mesh):
    ep_size, tp_size = mesh.devices.shape
    x_size = ep_size // 8
    split_mesh = Mesh(
        mesh.devices.reshape(x_size, ep_size // (2 * x_size), 2, tp_size), ("x", "y", "c", "tp")
    )
    ep = ("x", "y", "c")
    placed = (
        P(None, ep, "tp"),
        P(None, None, ep, "tp"),
        P(None, ep, None, "tp"),
        P(ep),
        P(None, (*ep, "tp"), None),
        P(),
        P("tp", ep),
        P(None, (*ep, "tp"), None),
        P(None, (*ep, "tp"), None),
        P((*ep, "tp"), None, None),
        P((*ep, "tp"), None, None),
        P((*ep, "tp"), None, None),
    )
    return jax.shard_map(
        per_device,
        mesh=split_mesh,
        in_specs=placed,
        out_specs=P(None, (*ep, "tp"), None),
        check_vma=False,
    )
```

```python
import jax
import jax.numpy as jnp
from jax import lax
from jax.sharding import Mesh, PartitionSpec as P

HEAD_SIZE = 128
TOPK = 8
SLOTS = 256
DECODE_STEPS = 3


masked_score = -1e30
norm_eps = 1e-06


def per_device(
    query,
    step_key_value,
    key_value_cache,
    lengths,
    hidden_in,
    norm_gain,
    w_out,
    routes,
    gate_scores,
    expert_gate,
    expert_up,
    expert_down,
):
    x_count = lax.axis_size("x")
    yc_count = lax.axis_size("y") * lax.axis_size("c")
    ep_count = x_count * yc_count
    tp_count = lax.axis_size("tp")
    steps = query.shape[0]
    row_dev = query.shape[1]
    row_own = hidden_in.shape[1]
    width = hidden_in.shape[2]
    heads_dev = query.shape[2] // HEAD_SIZE
    cache_len = key_value_cache.shape[2]
    expert_count = ep_count * tp_count * expert_gate.shape[0]
    capacity = SLOTS // expert_count
    score_scale = HEAD_SIZE ** (-0.5)
    stored_keys = key_value_cache[0]
    stored_values = key_value_cache[1]
    usable = jnp.arange(cache_len, dtype=jnp.int32)[None, :] < lengths[:, None]

    query_rows = query.reshape(steps, row_dev, heads_dev, HEAD_SIZE)
    incoming_keys = step_key_value[:, 0]
    incoming_values = step_key_value[:, 1]
    cache_scores = (
        jnp.einsum("srhd,rjd->srhj", query_rows, stored_keys, preferred_element_type=jnp.float32)
        * score_scale
    )
    cache_scores = jnp.where(usable[None, :, None, :], cache_scores, masked_score)
    fresh_scores = (
        jnp.einsum("srhd,jrd->srhj", query_rows, incoming_keys, preferred_element_type=jnp.float32)
        * score_scale
    )
    fresh_ok = (
        jnp.arange(steps, dtype=jnp.int32)[None, :] <= jnp.arange(steps, dtype=jnp.int32)[:, None]
    )
    fresh_scores = jnp.where(fresh_ok[:, None, None, :], fresh_scores, masked_score)
    scores = jnp.concatenate([cache_scores, fresh_scores], axis=-1)
    top = jnp.max(scores, axis=-1, keepdims=True)
    raised = jnp.exp(scores - top)
    probs = (raised / jnp.sum(raised, axis=-1, keepdims=True)).astype(jnp.bfloat16)
    attended = jnp.einsum(
        "srhj,rjd->srhd", probs[..., :cache_len], stored_values, preferred_element_type=jnp.float32
    )
    attended = attended + jnp.einsum(
        "srhj,jrd->srhd", probs[..., cache_len:], incoming_values, preferred_element_type=jnp.float32
    )
    attended = attended.astype(jnp.bfloat16).reshape(steps, row_dev, heads_dev * HEAD_SIZE)

    x_here = lax.axis_index("x")
    shifted = [w_out] + [
        lax.ppermute(w_out, "x", [(i, (i + k) % x_count) for i in range(x_count)])
        for k in range(1, x_count)
    ]
    order = (x_here - jnp.arange(x_count, dtype=jnp.int32)) % x_count
    w_cols = jnp.take(jnp.stack(shifted), order, axis=0, mode="clip")
    w_cols = jnp.transpose(w_cols, (1, 0, 2)).reshape(w_out.shape[0], -1)
    gathered = lax.all_gather(attended, ("y", "c"), axis=1, tiled=True)
    partial_sums = jnp.einsum(
        "srk,kc->src", gathered, w_cols, preferred_element_type=jnp.float32
    )
    grouped = partial_sums.astype(jnp.bfloat16).reshape(steps, yc_count * tp_count, row_own, -1)
    arrived_sums = lax.all_to_all(
        grouped, ("y", "c", "tp"), split_axis=1, concat_axis=1, tiled=True
    )
    arrived_sums = arrived_sums.reshape(steps, yc_count, tp_count, row_own, x_count, -1)
    summed = jnp.sum(arrived_sums.astype(jnp.float32), axis=2)
    projected = summed.astype(jnp.bfloat16)
    row_major = jnp.transpose(projected, (0, 2, 3, 1, 4)).reshape(steps, row_own, width)

    residual = hidden_in.astype(jnp.float32) + row_major.astype(jnp.float32)
    mean_square = jnp.mean(residual * residual, axis=-1, keepdims=True)
    normed = (residual * lax.rsqrt(mean_square + norm_eps) * norm_gain).astype(jnp.bfloat16)
    weights = gate_scores / jnp.sum(gate_scores, axis=-1, keepdims=True)

    slots_per = steps * capacity
    expert_ids = routes.reshape(steps, -1)
    assigned = expert_ids.shape[1]
    matches = (
        expert_ids[:, :, None] == jnp.arange(expert_count, dtype=jnp.int32)[None, None, :]
    ).astype(jnp.int32)
    earlier = jnp.cumsum(matches, axis=1) - matches
    slot_rank = jnp.sum(earlier * matches, axis=2)
    step_ids = jnp.arange(steps, dtype=jnp.int32)[:, None]
    slot_index = (expert_ids * slots_per + step_ids * capacity + slot_rank).reshape(-1)
    row_ids = (step_ids * row_own + jnp.arange(assigned, dtype=jnp.int32)[None, :] // TOPK).reshape(-1)
    empty = steps * row_own
    source_row = jnp.full((expert_count * slots_per,), empty, jnp.int32).at[slot_index].set(row_ids)
    blocks = width // 128
    padded = jnp.concatenate(
        [normed.reshape(steps * row_own, blocks, 128), jnp.zeros((1, blocks, 128), jnp.bfloat16)]
    )
    source_by_step = source_row.reshape(expert_count, steps, capacity)
    chunks = ((0, steps - 1), (steps - 1, steps)) if steps > 1 else ((0, steps),)
    group = ("x", "y", "c", "tp")
    picked = []
    for first, last in chunks:
        span = (last - first) * capacity
        wire_shape = (expert_count, span * blocks, 128)
        chunk_rows = source_by_step[:, first:last].reshape(-1)
        outgoing = jnp.take(padded, chunk_rows, axis=0, mode="clip").reshape(wire_shape)
        arrived = lax.all_to_all(outgoing, group, split_axis=0, concat_axis=0, tiled=True)
        flat_rows = arrived.reshape(-1, width)
        gate_act = jnp.dot(flat_rows, expert_gate[0], preferred_element_type=jnp.float32)
        up_act = jnp.dot(flat_rows, expert_up[0], preferred_element_type=jnp.float32)
        hidden = (jax.nn.silu(gate_act) * up_act).astype(jnp.bfloat16)
        expert_out = jnp.dot(
            hidden, expert_down[0], preferred_element_type=jnp.float32
        ).astype(jnp.bfloat16)
        returned = lax.all_to_all(
            expert_out.reshape(wire_shape), group, split_axis=0, concat_axis=0, tiled=True
        )
        returned = returned.reshape(expert_count * span, blocks, 128)
        local_slot = (
            expert_ids[first:last] * span
            + (step_ids[first:last] - first) * capacity
            + slot_rank[first:last]
        ).reshape(-1)
        picked.append(jnp.take(returned, local_slot, axis=0, mode="clip"))
    selected = jnp.concatenate(picked).astype(jnp.float32)
    selected = selected * weights.reshape(-1)[:, None, None]
    expert_mix = jnp.sum(selected.reshape(steps, row_own, TOPK, blocks, 128), axis=2)
    expert_mix = expert_mix.reshape(steps, row_own, width)
    return (residual + expert_mix).astype(jnp.bfloat16)


def solution(mesh):
    ep_size, tp_size = mesh.devices.shape
    x_size = ep_size // 8
    split_mesh = Mesh(
        mesh.devices.reshape(x_size, ep_size // (2 * x_size), 2, tp_size), ("x", "y", "c", "tp")
    )
    ep = ("x", "y", "c")
    placed = (
        P(None, ep, "tp"),
        P(None, None, ep, "tp"),
        P(None, ep, None, "tp"),
        P(ep),
        P(None, (*ep, "tp"), None),
        P(),
        P("tp", ep),
        P(None, (*ep, "tp"), None),
        P(None, (*ep, "tp"), None),
        P((*ep, "tp"), None, None),
        P((*ep, "tp"), None, None),
        P((*ep, "tp"), None, None),
    )
    return jax.shard_map(
        per_device,
        mesh=split_mesh,
        in_specs=placed,
        out_specs=P(None, (*ep, "tp"), None),
        check_vma=False,
    )
```

```python
import jax
import jax.numpy as jnp
from jax import lax
from jax.sharding import Mesh, PartitionSpec as P

HEAD_SIZE = 128
TOPK = 8
SLOTS = 256
DECODE_STEPS = 3


masked_score = -1e30
norm_eps = 1e-06


def per_device(
    query,
    step_key_value,
    key_value_cache,
    lengths,
    hidden_in,
    norm_gain,
    w_out,
    routes,
    gate_scores,
    expert_gate,
    expert_up,
    expert_down,
):
    x_count = lax.axis_size("x")
    yc_count = lax.axis_size("y") * lax.axis_size("c")
    ep_count = x_count * yc_count
    tp_count = lax.axis_size("tp")
    steps = query.shape[0]
    row_dev = query.shape[1]
    row_own = hidden_in.shape[1]
    width = hidden_in.shape[2]
    heads_dev = query.shape[2] // HEAD_SIZE
    cache_len = key_value_cache.shape[2]
    expert_count = ep_count * tp_count * expert_gate.shape[0]
    capacity = SLOTS // expert_count
    score_scale = HEAD_SIZE ** (-0.5)
    stored_keys = key_value_cache[0]
    stored_values = key_value_cache[1]
    usable = jnp.arange(cache_len, dtype=jnp.int32)[None, :] < lengths[:, None]

    query_rows = query.reshape(steps, row_dev, heads_dev, HEAD_SIZE)
    incoming_keys = step_key_value[:, 0]
    incoming_values = step_key_value[:, 1]
    cache_scores = (
        jnp.einsum("srhd,rjd->srhj", query_rows, stored_keys, preferred_element_type=jnp.float32)
        * score_scale
    )
    cache_scores = jnp.where(usable[None, :, None, :], cache_scores, masked_score)
    fresh_scores = (
        jnp.einsum("srhd,jrd->srhj", query_rows, incoming_keys, preferred_element_type=jnp.float32)
        * score_scale
    )
    fresh_ok = (
        jnp.arange(steps, dtype=jnp.int32)[None, :] <= jnp.arange(steps, dtype=jnp.int32)[:, None]
    )
    fresh_scores = jnp.where(fresh_ok[:, None, None, :], fresh_scores, masked_score)
    scores = jnp.concatenate([cache_scores, fresh_scores], axis=-1)
    top = jnp.max(scores, axis=-1, keepdims=True)
    raised = jnp.exp(scores - top)
    probs = (raised / jnp.sum(raised, axis=-1, keepdims=True)).astype(jnp.bfloat16)
    attended = jnp.einsum(
        "srhj,rjd->srhd", probs[..., :cache_len], stored_values, preferred_element_type=jnp.float32
    )
    attended = attended + jnp.einsum(
        "srhj,jrd->srhd", probs[..., cache_len:], incoming_values, preferred_element_type=jnp.float32
    )
    attended = attended.astype(jnp.bfloat16).reshape(steps, row_dev, heads_dev * HEAD_SIZE)

    x_here = lax.axis_index("x")
    shifted = [w_out] + [
        lax.ppermute(w_out, "x", [(i, (i + k) % x_count) for i in range(x_count)])
        for k in range(1, x_count)
    ]
    gathered = lax.all_gather(attended, ("y", "c"), axis=1, tiled=True)
    partial_sums = jnp.einsum(
        "srk,jkc->srjc", gathered, jnp.stack(shifted), preferred_element_type=jnp.float32
    )
    grouped = partial_sums.reshape(steps, yc_count * tp_count, row_own, -1)
    arrived_sums = lax.all_to_all(
        grouped, ("y", "c", "tp"), split_axis=1, concat_axis=1, tiled=True
    )
    arrived_sums = arrived_sums.reshape(steps, yc_count, tp_count, row_own, x_count, -1)
    summed = jnp.sum(arrived_sums, axis=2)
    order = (x_here - jnp.arange(x_count, dtype=jnp.int32)) % x_count
    summed = jnp.take(summed, order, axis=3, mode="clip")
    projected = summed.astype(jnp.bfloat16)
    row_major = jnp.transpose(projected, (0, 2, 3, 1, 4)).reshape(steps, row_own, width)

    residual = hidden_in.astype(jnp.float32) + row_major.astype(jnp.float32)
    mean_square = jnp.mean(residual * residual, axis=-1, keepdims=True)
    normed = (residual * lax.rsqrt(mean_square + norm_eps) * norm_gain).astype(jnp.bfloat16)
    weights = gate_scores / jnp.sum(gate_scores, axis=-1, keepdims=True)

    slots_per = steps * capacity
    expert_ids = routes.reshape(steps, -1)
    assigned = expert_ids.shape[1]
    matches = (
        expert_ids[:, :, None] == jnp.arange(expert_count, dtype=jnp.int32)[None, None, :]
    ).astype(jnp.int32)
    earlier = jnp.cumsum(matches, axis=1) - matches
    slot_rank = jnp.sum(earlier * matches, axis=2)
    step_ids = jnp.arange(steps, dtype=jnp.int32)[:, None]
    slot_index = (expert_ids * slots_per + step_ids * capacity + slot_rank).reshape(-1)
    row_ids = (step_ids * row_own + jnp.arange(assigned, dtype=jnp.int32)[None, :] // TOPK).reshape(-1)
    empty = steps * row_own
    source_row = jnp.full((expert_count * slots_per,), empty, jnp.int32).at[slot_index].set(row_ids)
    blocks = width // 128
    padded = jnp.concatenate(
        [normed.reshape(steps * row_own, blocks, 128), jnp.zeros((1, blocks, 128), jnp.bfloat16)]
    )
    source_by_step = source_row.reshape(expert_count, steps, capacity)
    chunks = ((0, steps - 1), (steps - 1, steps)) if steps > 1 else ((0, steps),)
    group = ("x", "y", "c", "tp")
    picked = []
    for first, last in chunks:
        span = (last - first) * capacity
        wire_shape = (expert_count, span * blocks, 128)
        chunk_rows = source_by_step[:, first:last].reshape(-1)
        outgoing = jnp.take(padded, chunk_rows, axis=0, mode="clip").reshape(wire_shape)
        arrived = lax.all_to_all(outgoing, group, split_axis=0, concat_axis=0, tiled=True)
        flat_rows = arrived.reshape(-1, width)
        gate_act = jnp.dot(flat_rows, expert_gate[0], preferred_element_type=jnp.float32)
        up_act = jnp.dot(flat_rows, expert_up[0], preferred_element_type=jnp.float32)
        hidden = (jax.nn.silu(gate_act) * up_act).astype(jnp.bfloat16)
        expert_out = jnp.dot(
            hidden, expert_down[0], preferred_element_type=jnp.float32
        ).astype(jnp.bfloat16)
        returned = lax.all_to_all(
            expert_out.reshape(wire_shape), group, split_axis=0, concat_axis=0, tiled=True
        )
        returned = returned.reshape(expert_count * span, blocks, 128)
        local_slot = (
            expert_ids[first:last] * span
            + (step_ids[first:last] - first) * capacity
            + slot_rank[first:last]
        ).reshape(-1)
        picked.append(jnp.take(returned, local_slot, axis=0, mode="clip"))
    selected = jnp.concatenate(picked).astype(jnp.float32)
    selected = selected * weights.reshape(-1)[:, None, None]
    expert_mix = jnp.sum(selected.reshape(steps, row_own, TOPK, blocks, 128), axis=2)
    expert_mix = expert_mix.reshape(steps, row_own, width)
    return (residual + expert_mix).astype(jnp.bfloat16)


def solution(mesh):
    ep_size, tp_size = mesh.devices.shape
    x_size = ep_size // 8
    split_mesh = Mesh(
        mesh.devices.reshape(x_size, ep_size // (2 * x_size), 2, tp_size), ("x", "y", "c", "tp")
    )
    ep = ("x", "y", "c")
    placed = (
        P(None, ep, "tp"),
        P(None, None, ep, "tp"),
        P(None, ep, None, "tp"),
        P(ep),
        P(None, (*ep, "tp"), None),
        P(),
        P("tp", ep),
        P(None, (*ep, "tp"), None),
        P(None, (*ep, "tp"), None),
        P((*ep, "tp"), None, None),
        P((*ep, "tp"), None, None),
        P((*ep, "tp"), None, None),
    )
    return jax.shard_map(
        per_device,
        mesh=split_mesh,
        in_specs=placed,
        out_specs=P(None, (*ep, "tp"), None),
        check_vma=False,
    )
```

```python
import jax
import jax.numpy as jnp
from jax import lax
from jax.sharding import Mesh, PartitionSpec as P

HEAD_SIZE = 128
TOPK = 8
SLOTS = 256
DECODE_STEPS = 3


masked_score = -1e30
norm_eps = 1e-06


def per_device(
    query,
    step_key_value,
    key_value_cache,
    lengths,
    hidden_in,
    norm_gain,
    w_out,
    routes,
    gate_scores,
    expert_gate,
    expert_up,
    expert_down,
):
    x_count = lax.axis_size("x")
    yc_count = lax.axis_size("y") * lax.axis_size("c")
    ep_count = x_count * yc_count
    tp_count = lax.axis_size("tp")
    steps = query.shape[0]
    row_dev = query.shape[1]
    row_own = hidden_in.shape[1]
    width = hidden_in.shape[2]
    heads_dev = query.shape[2] // HEAD_SIZE
    cache_len = key_value_cache.shape[2]
    expert_count = ep_count * tp_count * expert_gate.shape[0]
    capacity = SLOTS // expert_count
    score_scale = HEAD_SIZE ** (-0.5)
    stored_keys = key_value_cache[0]
    stored_values = key_value_cache[1]
    usable = jnp.arange(cache_len, dtype=jnp.int32)[None, :] < lengths[:, None]

    query_rows = query.reshape(steps, row_dev, heads_dev, HEAD_SIZE)
    incoming_keys = step_key_value[:, 0]
    incoming_values = step_key_value[:, 1]
    cache_scores = (
        jnp.einsum("srhd,rjd->srhj", query_rows, stored_keys, preferred_element_type=jnp.float32)
        * score_scale
    )
    cache_scores = jnp.where(usable[None, :, None, :], cache_scores, masked_score)
    fresh_scores = (
        jnp.einsum("srhd,jrd->srhj", query_rows, incoming_keys, preferred_element_type=jnp.float32)
        * score_scale
    )
    fresh_ok = (
        jnp.arange(steps, dtype=jnp.int32)[None, :] <= jnp.arange(steps, dtype=jnp.int32)[:, None]
    )
    fresh_scores = jnp.where(fresh_ok[:, None, None, :], fresh_scores, masked_score)
    scores = jnp.concatenate([cache_scores, fresh_scores], axis=-1)
    top = jnp.max(scores, axis=-1, keepdims=True)
    raised = jnp.exp(scores - top)
    probs = (raised / jnp.sum(raised, axis=-1, keepdims=True)).astype(jnp.bfloat16)
    attended = jnp.einsum(
        "srhj,rjd->srhd", probs[..., :cache_len], stored_values, preferred_element_type=jnp.float32
    )
    attended = attended + jnp.einsum(
        "srhj,jrd->srhd", probs[..., cache_len:], incoming_values, preferred_element_type=jnp.float32
    )
    attended = attended.astype(jnp.bfloat16).reshape(steps, row_dev, heads_dev * HEAD_SIZE)

    x_here = lax.axis_index("x")
    shifted = [w_out] + [
        lax.ppermute(w_out, "x", [(i, (i + k) % x_count) for i in range(x_count)])
        for k in range(1, x_count)
    ]
    gathered = lax.all_gather(attended, ("y", "c"), axis=1, tiled=True)
    partial_sums = jnp.einsum(
        "srk,jkc->srjc", gathered, jnp.stack(shifted), preferred_element_type=jnp.float32
    )
    grouped = partial_sums.reshape(steps, yc_count * tp_count, row_own, -1)
    arrived_sums = lax.all_to_all(
        grouped, ("y", "c", "tp"), split_axis=1, concat_axis=1, tiled=True
    )
    arrived_sums = arrived_sums.reshape(steps, yc_count, tp_count, row_own, x_count, -1)
    summed = jnp.sum(arrived_sums, axis=2)
    order = (x_here - jnp.arange(x_count, dtype=jnp.int32)) % x_count
    summed = jnp.take(summed, order, axis=3, mode="clip")
    projected = summed.astype(jnp.bfloat16)
    row_major = jnp.transpose(projected, (0, 2, 3, 1, 4)).reshape(steps, row_own, width)

    residual = hidden_in.astype(jnp.float32) + row_major.astype(jnp.float32)
    mean_square = jnp.mean(residual * residual, axis=-1, keepdims=True)
    normed = (residual * lax.rsqrt(mean_square + norm_eps) * norm_gain).astype(jnp.bfloat16)
    weights = gate_scores / jnp.sum(gate_scores, axis=-1, keepdims=True)

    slots_per = steps * capacity
    expert_ids = routes.reshape(steps, -1)
    assigned = expert_ids.shape[1]
    matches = (
        expert_ids[:, :, None] == jnp.arange(expert_count, dtype=jnp.int32)[None, None, :]
    ).astype(jnp.int32)
    earlier = jnp.cumsum(matches, axis=1) - matches
    slot_rank = jnp.sum(earlier * matches, axis=2)
    step_ids = jnp.arange(steps, dtype=jnp.int32)[:, None]
    slot_index = (expert_ids * slots_per + step_ids * capacity + slot_rank).reshape(-1)
    row_ids = (step_ids * row_own + jnp.arange(assigned, dtype=jnp.int32)[None, :] // TOPK).reshape(-1)
    empty = steps * row_own
    source_row = jnp.full((expert_count * slots_per,), empty, jnp.int32).at[slot_index].set(row_ids)
    blocks = width // 128
    padded = jnp.concatenate(
        [normed.reshape(steps * row_own, blocks, 128), jnp.zeros((1, blocks, 128), jnp.bfloat16)]
    )
    source_by_slot = source_row.reshape(expert_count, slots_per)
    half = slots_per // 2
    chunks = ((0, half), (half, slots_per))
    group = ("x", "y", "c", "tp")
    slot_of = (step_ids * capacity + slot_rank).reshape(-1)
    picked = []
    for first, last in chunks:
        span = last - first
        wire_shape = (expert_count, span * blocks, 128)
        chunk_rows = source_by_slot[:, first:last].reshape(-1)
        outgoing = jnp.take(padded, chunk_rows, axis=0, mode="clip").reshape(wire_shape)
        arrived = lax.all_to_all(outgoing, group, split_axis=0, concat_axis=0, tiled=True)
        flat_rows = arrived.reshape(-1, width)
        gate_act = jnp.dot(flat_rows, expert_gate[0], preferred_element_type=jnp.float32)
        up_act = jnp.dot(flat_rows, expert_up[0], preferred_element_type=jnp.float32)
        hidden = (jax.nn.silu(gate_act) * up_act).astype(jnp.bfloat16)
        expert_out = jnp.dot(
            hidden, expert_down[0], preferred_element_type=jnp.float32
        ).astype(jnp.bfloat16)
        returned = lax.all_to_all(
            expert_out.reshape(wire_shape), group, split_axis=0, concat_axis=0, tiled=True
        )
        returned = returned.reshape(expert_count * span, blocks, 128)
        local_slot = expert_ids.reshape(-1) * span + jnp.clip(slot_of - first, 0, span - 1)
        picked.append(jnp.take(returned, local_slot, axis=0, mode="clip"))
    in_second = (slot_of >= half)[:, None, None]
    selected = jnp.where(in_second, picked[1], picked[0]).astype(jnp.float32)
    selected = selected * weights.reshape(-1)[:, None, None]
    expert_mix = jnp.sum(selected.reshape(steps, row_own, TOPK, blocks, 128), axis=2)
    expert_mix = expert_mix.reshape(steps, row_own, width)
    return (residual + expert_mix).astype(jnp.bfloat16)


def solution(mesh):
    ep_size, tp_size = mesh.devices.shape
    x_size = ep_size // 8
    split_mesh = Mesh(
        mesh.devices.reshape(x_size, ep_size // (2 * x_size), 2, tp_size), ("x", "y", "c", "tp")
    )
    ep = ("x", "y", "c")
    placed = (
        P(None, ep, "tp"),
        P(None, None, ep, "tp"),
        P(None, ep, None, "tp"),
        P(ep),
        P(None, (*ep, "tp"), None),
        P(),
        P("tp", ep),
        P(None, (*ep, "tp"), None),
        P(None, (*ep, "tp"), None),
        P((*ep, "tp"), None, None),
        P((*ep, "tp"), None, None),
        P((*ep, "tp"), None, None),
    )
    return jax.shard_map(
        per_device,
        mesh=split_mesh,
        in_specs=placed,
        out_specs=P(None, (*ep, "tp"), None),
        check_vma=False,
    )
```

```python
import jax
import jax.numpy as jnp
from jax import lax
from jax.sharding import Mesh, PartitionSpec as P

HEAD_SIZE = 128
TOPK = 8
SLOTS = 256
DECODE_STEPS = 3


masked_score = -1e30
norm_eps = 1e-06


def per_device(
    query,
    step_key_value,
    key_value_cache,
    lengths,
    hidden_in,
    norm_gain,
    w_out,
    routes,
    gate_scores,
    expert_gate,
    expert_up,
    expert_down,
):
    x_count = lax.axis_size("x")
    yc_count = lax.axis_size("y") * lax.axis_size("c")
    ep_count = x_count * yc_count
    tp_count = lax.axis_size("tp")
    steps = query.shape[0]
    row_dev = query.shape[1]
    row_own = hidden_in.shape[1]
    width = hidden_in.shape[2]
    heads_dev = query.shape[2] // HEAD_SIZE
    cache_len = key_value_cache.shape[2]
    expert_count = ep_count * tp_count * expert_gate.shape[0]
    capacity = SLOTS // expert_count
    score_scale = HEAD_SIZE ** (-0.5)
    stored_keys = key_value_cache[0]
    stored_values = key_value_cache[1]
    usable = jnp.arange(cache_len, dtype=jnp.int32)[None, :] < lengths[:, None]

    query_rows = query.reshape(steps, row_dev, heads_dev, HEAD_SIZE)
    all_keys = jnp.concatenate([stored_keys, jnp.transpose(step_key_value[:, 0], (1, 0, 2))], axis=1)
    all_values = jnp.concatenate(
        [stored_values, jnp.transpose(step_key_value[:, 1], (1, 0, 2))], axis=1
    )
    scores = (
        jnp.einsum("srhd,rjd->srhj", query_rows, all_keys, preferred_element_type=jnp.float32)
        * score_scale
    )
    fresh_ok = (
        jnp.arange(steps, dtype=jnp.int32)[None, :] <= jnp.arange(steps, dtype=jnp.int32)[:, None]
    )
    allowed = jnp.concatenate(
        [
            jnp.broadcast_to(usable[None], (steps, row_dev, cache_len)),
            jnp.broadcast_to(fresh_ok[:, None, :], (steps, row_dev, steps)),
        ],
        axis=-1,
    )
    scores = jnp.where(allowed[:, :, None, :], scores, masked_score)
    top = jnp.max(scores, axis=-1, keepdims=True)
    raised = jnp.exp(scores - top)
    probs = (raised / jnp.sum(raised, axis=-1, keepdims=True)).astype(jnp.bfloat16)
    attended = jnp.einsum(
        "srhj,rjd->srhd", probs, all_values, preferred_element_type=jnp.float32
    )
    attended = attended.astype(jnp.bfloat16).reshape(steps, row_dev, heads_dev * HEAD_SIZE)

    x_here = lax.axis_index("x")
    shifted = [w_out] + [
        lax.ppermute(w_out, "x", [(i, (i + k) % x_count) for i in range(x_count)])
        for k in range(1, x_count)
    ]
    gathered = lax.all_gather(attended, ("y", "c"), axis=1, tiled=True)
    partial_sums = jnp.einsum(
        "srk,jkc->srjc", gathered, jnp.stack(shifted), preferred_element_type=jnp.float32
    )
    grouped = partial_sums.reshape(steps, yc_count * tp_count, row_own, -1)
    arrived_sums = lax.all_to_all(
        grouped, ("y", "c", "tp"), split_axis=1, concat_axis=1, tiled=True
    )
    arrived_sums = arrived_sums.reshape(steps, yc_count, tp_count, row_own, x_count, -1)
    summed = jnp.sum(arrived_sums, axis=2)
    order = (x_here - jnp.arange(x_count, dtype=jnp.int32)) % x_count
    summed = jnp.take(summed, order, axis=3, mode="clip")
    projected = summed.astype(jnp.bfloat16)
    row_major = jnp.transpose(projected, (0, 2, 3, 1, 4)).reshape(steps, row_own, width)

    residual = hidden_in.astype(jnp.float32) + row_major.astype(jnp.float32)
    mean_square = jnp.mean(residual * residual, axis=-1, keepdims=True)
    normed = (residual * lax.rsqrt(mean_square + norm_eps) * norm_gain).astype(jnp.bfloat16)
    weights = gate_scores / jnp.sum(gate_scores, axis=-1, keepdims=True)

    slots_per = steps * capacity
    expert_ids = routes.reshape(steps, -1)
    assigned = expert_ids.shape[1]
    matches = (
        expert_ids[:, :, None] == jnp.arange(expert_count, dtype=jnp.int32)[None, None, :]
    ).astype(jnp.int32)
    earlier = jnp.cumsum(matches, axis=1) - matches
    slot_rank = jnp.sum(earlier * matches, axis=2)
    step_ids = jnp.arange(steps, dtype=jnp.int32)[:, None]
    slot_index = (expert_ids * slots_per + step_ids * capacity + slot_rank).reshape(-1)
    row_ids = (step_ids * row_own + jnp.arange(assigned, dtype=jnp.int32)[None, :] // TOPK).reshape(-1)
    empty = steps * row_own
    source_row = jnp.full((expert_count * slots_per,), empty, jnp.int32).at[slot_index].set(row_ids)
    blocks = width // 128
    padded = jnp.concatenate(
        [normed.reshape(steps * row_own, blocks, 128), jnp.zeros((1, blocks, 128), jnp.bfloat16)]
    )
    source_by_slot = source_row.reshape(expert_count, slots_per)
    half = slots_per // 2
    chunks = ((0, half), (half, slots_per))
    group = ("x", "y", "c", "tp")
    slot_of = (step_ids * capacity + slot_rank).reshape(-1)
    picked = []
    for first, last in chunks:
        span = last - first
        wire_shape = (expert_count, span * blocks, 128)
        chunk_rows = source_by_slot[:, first:last].reshape(-1)
        outgoing = jnp.take(padded, chunk_rows, axis=0, mode="clip").reshape(wire_shape)
        arrived = lax.all_to_all(outgoing, group, split_axis=0, concat_axis=0, tiled=True)
        flat_rows = arrived.reshape(-1, width)
        gate_act = jnp.dot(flat_rows, expert_gate[0], preferred_element_type=jnp.float32)
        up_act = jnp.dot(flat_rows, expert_up[0], preferred_element_type=jnp.float32)
        hidden = (jax.nn.silu(gate_act) * up_act).astype(jnp.bfloat16)
        expert_out = jnp.dot(
            hidden, expert_down[0], preferred_element_type=jnp.float32
        ).astype(jnp.bfloat16)
        returned = lax.all_to_all(
            expert_out.reshape(wire_shape), group, split_axis=0, concat_axis=0, tiled=True
        )
        returned = returned.reshape(expert_count * span, blocks, 128)
        local_slot = expert_ids.reshape(-1) * span + jnp.clip(slot_of - first, 0, span - 1)
        picked.append(jnp.take(returned, local_slot, axis=0, mode="clip"))
    in_second = (slot_of >= half)[:, None, None]
    selected = jnp.where(in_second, picked[1], picked[0]).astype(jnp.float32)
    selected = selected * weights.reshape(-1)[:, None, None]
    expert_mix = jnp.sum(selected.reshape(steps, row_own, TOPK, blocks, 128), axis=2)
    expert_mix = expert_mix.reshape(steps, row_own, width)
    return (residual + expert_mix).astype(jnp.bfloat16)


def solution(mesh):
    ep_size, tp_size = mesh.devices.shape
    x_size = ep_size // 8
    split_mesh = Mesh(
        mesh.devices.reshape(x_size, ep_size // (2 * x_size), 2, tp_size), ("x", "y", "c", "tp")
    )
    ep = ("x", "y", "c")
    placed = (
        P(None, ep, "tp"),
        P(None, None, ep, "tp"),
        P(None, ep, None, "tp"),
        P(ep),
        P(None, (*ep, "tp"), None),
        P(),
        P("tp", ep),
        P(None, (*ep, "tp"), None),
        P(None, (*ep, "tp"), None),
        P((*ep, "tp"), None, None),
        P((*ep, "tp"), None, None),
        P((*ep, "tp"), None, None),
    )
    return jax.shard_map(
        per_device,
        mesh=split_mesh,
        in_specs=placed,
        out_specs=P(None, (*ep, "tp"), None),
        check_vma=False,
    )
```
